512 devices in a mesh: seq: 64 (over x, z), head: 8 (over y, core).
Axes of the slice: x: 4, y: 4, z: 16, core: 2. Of those that a mesh axis runs over, the one named last changes fastest.
Arguments:
- queries: bfloat16 [32768, 8192], P(('seq', 'head')), may hold values from -9 to 9
- keys: bfloat16 [32768, 1024], P(('seq', 'head')), may hold values from -9 to 9
- values: bfloat16 [32768, 1024], P(('seq', 'head')), may hold values from -6 to 6
- prefix_keys: bfloat16 [131072, 1024], P('seq', 'head'), may hold values from -6 to 6
- prefix_values: bfloat16 [131072, 1024], P('seq', 'head'), may hold values from -6 to 6
- roles: int32 [64], P('head'), may hold values from 0 to 1, as said below
- columns: int32 [64, 6], P('head'), may hold values from 0 to 2015, as said below
- col_count: int32 [64], P('head'), may hold values from 1 to 6, as said below
- diagonals: int32 [64, 4], P('head'), may hold values from 0 to 7, as said below
Outputs:
- attended: bfloat16 [32768, 8192], P('seq', 'head')
The draws below stay inside these ranges and needn't reach their ends.
Inputs may be any that keep to these rules, and one draw needn't show every extreme that they name: `roles`: 1 marks a retrieval head, 0 a passing head; at most 4 retrieval heads share one key-value head, and some key-value head has exactly 4. `columns`: prefix block indices, blocks of 64 cache rows, distinct within a head. `col_count`: some retrieval head uses all 6 of its column blocks. `diagonals`: distinct within a head; the first offset of every head is 0.
All inputs are finite; a program needn't handle non-finite values.
Results may differ from the reference program's by a relative error of at most 0.0049.
Values may be sent and summed in bfloat16 or wider, within the bound.
No kernel may reach another device: no remote copies, remote signals or barrier semaphores. Data moves between devices by JAX's collectives and lax.ppermute only.
A program may use at most 64 MiB of HBM per device.

```python
import math
import jax
import jax.numpy as jnp
from jax import lax

QUERY_HEADS = 64
KEY_VALUE_HEADS = 8
HEAD_SIZE = 128
P_DEV = 2048
SINK = 128
WIN = 512
BLK = 64
VB = 6
NSL = 4
MAX_RETRIEVERS = 4
SPAN_TOKENS = 32768
PREFIX_TOKENS = 131072


def draw_queries(key, part):
    drawn_random = jax.random.fold_in(key, 3)
    final_output = jnp.clip(2.0 * jax.random.normal(drawn_random, (SPAN_TOKENS, QUERY_HEADS * HEAD_SIZE), jnp.float32), -8.0, 8.0)
    return final_output.astype(jnp.bfloat16)


def draw_keys(key, part):
    drawn_random = jax.random.fold_in(key, 5)
    final_output = jnp.clip(jax.random.normal(drawn_random, (SPAN_TOKENS, KEY_VALUE_HEADS * HEAD_SIZE), jnp.float32), -4.0, 4.0)
    return final_output.astype(jnp.bfloat16)


def role_table(key):
    count_random, pinned_random, score_random = jax.random.split(jax.random.fold_in(key, 21), 3)
    group_share = QUERY_HEADS // KEY_VALUE_HEADS
    count_list = jax.random.randint(count_random, (KEY_VALUE_HEADS,), 0, MAX_RETRIEVERS + 1)
    pinned_choice = jax.random.randint(pinned_random, (), 0, KEY_VALUE_HEADS)
    count_list = jnp.where(jnp.arange(KEY_VALUE_HEADS) == pinned_choice, MAX_RETRIEVERS, count_list)
    score_matrix = jax.random.randint(score_random, (KEY_VALUE_HEADS, group_share), 0, 1 << 20) * group_share + jnp.arange(group_share)[None, :]
    ranking_lookup = jnp.argsort(jnp.argsort(score_matrix, axis=1), axis=1)
    chosen = ranking_lookup < count_list[:, None]
    front_entries = (ranking_lookup == 0) & (jnp.arange(KEY_VALUE_HEADS) == pinned_choice)[:, None]
    return (chosen.reshape(QUERY_HEADS).astype(jnp.int32), front_entries.reshape(QUERY_HEADS))


def draw_roles(key, part):
    chosen, front_entries = role_table(key)
    return chosen


def draw_col_count(key, part):
    chosen, front_entries = role_table(key)
    drawn = jax.random.randint(jax.random.fold_in(key, 23), (QUERY_HEADS,), 1, VB + 1)
    return jnp.where(front_entries, VB, drawn).astype(jnp.int32)


def draw_columns(key, part):
    allowed_blocks = (PREFIX_TOKENS - P_DEV) // BLK
    head_keys = jax.random.split(jax.random.fold_in(key, 31), QUERY_HEADS)

    def pick_blocks(head_key):
        return jax.random.permutation(head_key, allowed_blocks)[:VB]
    return jax.vmap(pick_blocks)(head_keys).astype(jnp.int32)


def draw_diagonals(key, part):
    head_keys = jax.random.split(jax.random.fold_in(key, 41), QUERY_HEADS)

    def pick_offsets(head_key):
        return jax.random.permutation(head_key, WIN // BLK - 1)[:NSL - 1] + 1
    others = jax.vmap(pick_offsets)(head_keys)
    return jnp.concatenate([jnp.zeros((QUERY_HEADS, 1), jnp.int32), others.astype(jnp.int32)], 1)


def block_scale(key, shape, cuts, low, largest):
    factor_of = 1.0
    for dim, blocks in cuts:
        heights = jax.random.uniform(jax.random.fold_in(jax.random.fold_in(key, 6), dim), (blocks,), jnp.float32, low / len(cuts), largest / len(cuts))
        factor_of = factor_of * jnp.repeat(jnp.exp(heights), shape[dim] // blocks).reshape((-1,) + (1,) * (len(shape) - 1 - dim))
    return factor_of


def gaussian(rng, shape, spread, limit, cuts=(), kind=jnp.bfloat16):
    values = jax.random.normal(rng, shape, jnp.float32) * spread
    if len(cuts) > 0:
        values = block_scale(rng, shape, cuts, -0.22, 0.18) * values
    return jnp.clip(values, min=-limit, max=limit).astype(kind)


def setup_inputs(seed: int = 0) -> dict:
    streams_of = jax.random.split(jax.random.key(seed), 10)
    return {
        "queries": draw_queries(jax.random.fold_in(streams_of[9], 71), 0),
        "keys": draw_keys(jax.random.fold_in(streams_of[9], 71), 0),
        "values": gaussian(streams_of[2], (SPAN_TOKENS, KEY_VALUE_HEADS * HEAD_SIZE), 1.0, 6.0, ((0, 512),)),
        "prefix_keys": gaussian(streams_of[3], (PREFIX_TOKENS, KEY_VALUE_HEADS * HEAD_SIZE), 1.0, 6.0, ((0, 64), (1, 8))),
        "prefix_values": gaussian(streams_of[4], (PREFIX_TOKENS, KEY_VALUE_HEADS * HEAD_SIZE), 1.0, 6.0, ((0, 64), (1, 8))),
        "roles": draw_roles(jax.random.fold_in(streams_of[9], 71), 0),
        "columns": draw_columns(jax.random.fold_in(streams_of[9], 71), 0),
        "col_count": draw_col_count(jax.random.fold_in(streams_of[9], 71), 0),
        "diagonals": draw_diagonals(jax.random.fold_in(streams_of[9], 71), 0),
    }


def masked_softmax(score_matrix, allowed):
    row_max = lax.optimization_barrier(jnp.max(jnp.where(allowed, score_matrix, -jnp.inf), axis=-1, keepdims=True))
    expo = jnp.where(allowed, jnp.exp(score_matrix - row_max), 0.0)
    total = lax.optimization_barrier(jnp.sum(expo, axis=-1, keepdims=True))
    return (expo / total).astype(jnp.bfloat16)

def passing(q_head, k_head, v_head):
    scaling = 1.0 / math.sqrt(HEAD_SIZE)
    offset_grid = jnp.arange(2 * WIN)[None, :] - jnp.arange(WIN)[:, None]
    band_ok = (offset_grid >= 1) & (offset_grid <= WIN)
    allowed = jnp.concatenate([jnp.ones((WIN, SINK), dtype=jnp.bool_), band_ok], 1)
    sink_k = k_head[:SINK]
    sink_v = v_head[:SINK]

    def one_block(which):
        q_rows = lax.dynamic_slice_in_dim(q_head, (which * WIN).astype(jnp.int32), WIN, 0)
        start = (PREFIX_TOKENS - WIN + which * WIN).astype(jnp.int32)
        band_k = lax.dynamic_slice_in_dim(k_head, start, 2 * WIN, 0)
        band_v = lax.dynamic_slice_in_dim(v_head, start, 2 * WIN, 0)
        keys_here = jnp.concatenate([sink_k, band_k], 0)
        vals_here = jnp.concatenate([sink_v, band_v], 0)
        score_matrix = jnp.dot(q_rows, keys_here.T, preferred_element_type=jnp.float32) * scaling
        probs = masked_softmax(score_matrix, allowed)
        return jnp.dot(probs, vals_here, preferred_element_type=jnp.float32)
    final_output = lax.map(one_block, jnp.arange(SPAN_TOKENS // WIN, dtype=jnp.int32))
    return final_output.reshape(SPAN_TOKENS, HEAD_SIZE)

def retrieval(q_head, k_head, v_head, cols, count_used, offsets_d):
    scaling = 1.0 / math.sqrt(HEAD_SIZE)
    vert_k = k_head[:PREFIX_TOKENS].reshape(PREFIX_TOKENS // BLK, BLK, HEAD_SIZE)[cols].reshape(VB * BLK, HEAD_SIZE)
    vert_v = v_head[:PREFIX_TOKENS].reshape(PREFIX_TOKENS // BLK, BLK, HEAD_SIZE)[cols].reshape(VB * BLK, HEAD_SIZE)
    key_blocks = k_head.reshape((PREFIX_TOKENS + SPAN_TOKENS) // BLK, BLK, HEAD_SIZE)
    val_blocks = v_head.reshape((PREFIX_TOKENS + SPAN_TOKENS) // BLK, BLK, HEAD_SIZE)
    per_rows = WIN // BLK
    vert_ok = jnp.arange(VB * BLK) // BLK < count_used
    within = jnp.arange(BLK)[None, :] <= jnp.arange(BLK)[:, None]
    slash_ok = (offsets_d[:, None, None] > 0) | within[None, :, :]
    slash_ok = jnp.transpose(slash_ok, (1, 0, 2)).reshape(BLK, NSL * BLK)
    allowed = jnp.concatenate([jnp.broadcast_to(vert_ok[None, :], (BLK, VB * BLK)), slash_ok], 1)

    def one_block(which):
        q_rows = lax.dynamic_slice_in_dim(q_head, (which * WIN).astype(jnp.int32), WIN, 0)
        picks = (PREFIX_TOKENS // BLK + which * per_rows + jnp.arange(per_rows))[:, None] - offsets_d[None, :]
        slash_k = key_blocks[picks].reshape(per_rows, NSL * BLK, HEAD_SIZE)
        slash_v = val_blocks[picks].reshape(per_rows, NSL * BLK, HEAD_SIZE)
        q_blocks = q_rows.reshape(per_rows, BLK, HEAD_SIZE)
        vert_scores = jnp.dot(q_rows, vert_k.T, preferred_element_type=jnp.float32) * scaling
        vert_scores = vert_scores.reshape(per_rows, BLK, VB * BLK)
        slash_scores = jnp.einsum('nqd,nkd->nqk', q_blocks.astype(jnp.float32), slash_k.astype(jnp.float32)) * scaling
        score_matrix = jnp.concatenate([vert_scores, slash_scores], -1)
        probs = masked_softmax(score_matrix, allowed[None, :, :])
        vert_part = jnp.dot(probs[:, :, :VB * BLK].reshape(WIN, VB * BLK), vert_v, preferred_element_type=jnp.float32)
        slash_part = jnp.einsum('nqk,nkd->nqd', probs[:, :, VB * BLK:].astype(jnp.float32), slash_v.astype(jnp.float32))
        return vert_part + slash_part.reshape(WIN, HEAD_SIZE)
    final_output = lax.map(one_block, jnp.arange(SPAN_TOKENS // WIN, dtype=jnp.int32))
    return final_output.reshape(SPAN_TOKENS, HEAD_SIZE)

def reference(queries, keys, values, prefix_keys, prefix_values, roles, columns, col_count, diagonals):
    all_keys = jnp.concatenate([prefix_keys, keys], 0)
    all_values = jnp.concatenate([prefix_values, values], 0)
    group_share = QUERY_HEADS // KEY_VALUE_HEADS

    def one_head(head_index):
        kv_head = head_index // group_share
        q_head = lax.dynamic_slice_in_dim(queries, (head_index * HEAD_SIZE).astype(jnp.int32), HEAD_SIZE, 1)
        k_head = lax.dynamic_slice_in_dim(all_keys, (kv_head * HEAD_SIZE).astype(jnp.int32), HEAD_SIZE, 1)
        v_head = lax.dynamic_slice_in_dim(all_values, (kv_head * HEAD_SIZE).astype(jnp.int32), HEAD_SIZE, 1)
        final_output = lax.cond(roles[head_index] == 1, lambda: retrieval(q_head, k_head, v_head, columns[head_index], col_count[head_index], diagonals[head_index]), lambda: passing(q_head, k_head, v_head))
        return final_output.astype(jnp.bfloat16)
    per_head = lax.map(one_head, jnp.arange(QUERY_HEADS, dtype=jnp.int32))
    return jnp.transpose(per_head, (1, 0, 2)).reshape(SPAN_TOKENS, QUERY_HEADS * HEAD_SIZE)
```

```python
import functools
import math

import jax
import jax.numpy as jnp
from jax import lax
from jax.experimental import pallas as pl
from jax.experimental.pallas import tpu as pltpu
from jax.sharding import PartitionSpec as P

QUERY_HEADS = 64
KEY_VALUE_HEADS = 8
HEAD_SIZE = 128
SINK = 128
WIN = 512
BLK = 64
VB = 6
NSL = 4
MAX_RETRIEVERS = 4


def shifted(block, axis, distance):
    devices = range(lax.axis_size(axis))
    route = [((i - distance) % len(devices), i) for i in devices]
    return lax.ppermute(block, axis, route)


def attend_kernel(roles_ref, slot_ref, count_ref, diag_ref,
                  q_ref, prev_ref, own_ref, vk_ref, vv_ref, sk_ref, sv_ref, o_ref):
    h = pl.program_id(0)
    rows = q_ref.shape[0]
    scaling = 1.0 / math.sqrt(HEAD_SIZE)
    q = q_ref[...]
    dims = (((1,), (1,)), ((), ()))

    def scores(keys):
        return lax.dot_general(q, keys, dims, preferred_element_type=jnp.float32) * scaling

    s_prev = scores(prev_ref[0])
    s_own = scores(own_ref[0])
    row = lax.broadcasted_iota(jnp.int32, (rows, rows), 0)
    col = lax.broadcasted_iota(jnp.int32, (rows, rows), 1)

    def finish(s_side, ok_side, v_side, ok_prev, ok_own):
        neg = -jnp.inf
        m_side = jnp.max(jnp.where(ok_side, s_side, neg), axis=1, keepdims=True)
        m_prev = jnp.max(jnp.where(ok_prev, s_prev, neg), axis=1, keepdims=True)
        m_own = jnp.max(jnp.where(ok_own, s_own, neg), axis=1, keepdims=True)
        m = jnp.maximum(jnp.maximum(m_side, m_prev), m_own)
        e_side = jnp.where(ok_side, jnp.exp(s_side - m), 0.0)
        e_prev = jnp.where(ok_prev, jnp.exp(s_prev - m), 0.0)
        e_own = jnp.where(ok_own, jnp.exp(s_own - m), 0.0)
        total = (jnp.sum(e_side, axis=1, keepdims=True)
                 + jnp.sum(e_prev, axis=1, keepdims=True)
                 + jnp.sum(e_own, axis=1, keepdims=True))
        p_side = (e_side / total).astype(jnp.bfloat16)
        p_prev = (e_prev / total).astype(jnp.bfloat16)
        p_own = (e_own / total).astype(jnp.bfloat16)
        out = jnp.dot(p_side, v_side, preferred_element_type=jnp.float32)
        out = out + jnp.dot(p_prev, prev_ref[1], preferred_element_type=jnp.float32)
        out = out + jnp.dot(p_own, own_ref[1], preferred_element_type=jnp.float32)
        o_ref[...] = out.astype(o_ref.dtype)

    @pl.when(roles_ref[h] != 1)
    def _():
        s_side = scores(sk_ref[...])
        ok_side = jnp.ones(s_side.shape, jnp.bool_)
        finish(s_side, ok_side, sv_ref[...], col > row, col <= row)

    @pl.when(roles_ref[h] == 1)
    def _():
        s_side = scores(vk_ref[...])
        side_col = lax.broadcasted_iota(jnp.int32, s_side.shape, 1)
        ok_side = side_col // BLK < count_ref[h]
        rel_prev = row // BLK + rows // BLK - col // BLK
        rel_own = row // BLK - col // BLK
        ok_prev = jnp.zeros((rows, rows), jnp.bool_)
        ok_own = jnp.zeros((rows, rows), jnp.bool_)
        for d in range(NSL):
            off = diag_ref[h * NSL + d]
            ok_prev = ok_prev | (rel_prev == off)
            ok_own = ok_own | ((rel_own == off) & ((off > 0) | (col <= row)))
        finish(s_side, ok_side, vv_ref[...], ok_prev, ok_own)


def attend(roles_l, slot_l, count_l, diag_l, q_local, prev_kv, own_kv, side):
    rows = q_local.shape[0]
    heads = q_local.shape[1] // HEAD_SIZE
    vrows = VB * BLK
    sink_block = MAX_RETRIEVERS * vrows // SINK
    grid_spec = pltpu.PrefetchScalarGridSpec(
        num_scalar_prefetch=4,
        grid=(heads,),
        in_specs=[
            pl.BlockSpec((rows, HEAD_SIZE), lambda h, *_: (0, h)),
            pl.BlockSpec((2, rows, HEAD_SIZE), lambda h, *_: (0, 0, 0)),
            pl.BlockSpec((2, rows, HEAD_SIZE), lambda h, *_: (0, 0, 0)),
            pl.BlockSpec((None, vrows, HEAD_SIZE), lambda h, r, s, *_: (0, s[h], 0)),
            pl.BlockSpec((None, vrows, HEAD_SIZE), lambda h, r, s, *_: (1, s[h], 0)),
            pl.BlockSpec((None, SINK, HEAD_SIZE), lambda h, *_: (0, sink_block, 0)),
            pl.BlockSpec((None, SINK, HEAD_SIZE), lambda h, *_: (1, sink_block, 0)),
        ],
        out_specs=pl.BlockSpec((rows, HEAD_SIZE), lambda h, *_: (0, h)),
    )
    return pl.pallas_call(
        attend_kernel,
        grid_spec=grid_spec,
        out_shape=jax.ShapeDtypeStruct(q_local.shape, jnp.bfloat16),
    )(roles_l, slot_l, count_l, diag_l, q_local, prev_kv, own_kv, side, side, side, side)


def shards(queries, keys, values, prefix_keys, prefix_values, roles, columns, col_count, diagonals):
    seq_devices = lax.axis_size("seq")
    my_seq = lax.axis_index("seq")
    cache_rows = prefix_keys.shape[0]
    blocks_dev = cache_rows // BLK
    heads = roles.shape[0]

    is_ret = roles == 1
    slot = jnp.cumsum(is_ret.astype(jnp.int32)) - 1
    match = is_ret[None, :] & (slot[None, :] == jnp.arange(MAX_RETRIEVERS, dtype=jnp.int32)[:, None])
    head_of_slot = jnp.argmax(match, axis=1)
    cols_s = columns[head_of_slot]
    owner = cols_s // blocks_dev
    local_block = cols_s - owner * blocks_dev
    mine = (owner == my_seq)[:, :, None, None]
    kv_blocks = jnp.stack([prefix_keys, prefix_values], 0).reshape(2, blocks_dev, BLK, HEAD_SIZE)
    pieces = kv_blocks[:, local_block]
    pieces = jnp.where(mine[None], pieces, jnp.zeros_like(pieces))
    pieces = pieces.reshape(2, MAX_RETRIEVERS * VB * BLK, HEAD_SIZE)
    sink = jnp.stack([prefix_keys[:SINK], prefix_values[:SINK]], 0)
    sink = jnp.where(my_seq == 0, sink, jnp.zeros_like(sink))
    side = lax.psum(jnp.concatenate([pieces, sink], 1), "seq")

    q_local = lax.all_to_all(queries, "head", split_axis=1, concat_axis=0, tiled=True)
    kv = jnp.stack([keys, values], 0)
    kv_local = lax.all_to_all(kv, "head", split_axis=2, concat_axis=1, tiled=True)
    tail_cache = jnp.stack([prefix_keys[cache_rows - WIN:], prefix_values[cache_rows - WIN:]], 0)
    outgoing = jnp.where(my_seq == seq_devices - 1, tail_cache, kv_local)
    prev_kv = shifted(outgoing, "seq", 1)

    slot_l = jnp.where(is_ret, slot, 0).astype(jnp.int32)
    return attend(
        roles.astype(jnp.int32),
        slot_l,
        col_count.astype(jnp.int32),
        diagonals.reshape(heads * NSL).astype(jnp.int32),
        q_local,
        prev_kv,
        kv_local,
        side,
    )


def solution(mesh):
    placed = (
        P(("seq", "head"), None),
        P(("seq", "head"), None),
        P(("seq", "head"), None),
        P("seq", "head"),
        P("seq", "head"),
        P("head"),
        P("head", None),
        P("head"),
        P("head", None),
    )
    return jax.shard_map(
        shards, mesh=mesh, in_specs=placed, out_specs=P("seq", "head"), check_vma=False
    )
```

```python
import functools
import math

import jax
import jax.numpy as jnp
from jax import lax
from jax.experimental import pallas as pl
from jax.experimental.pallas import tpu as pltpu
from jax.sharding import PartitionSpec as P

QUERY_HEADS = 64
KEY_VALUE_HEADS = 8
HEAD_SIZE = 128
SINK = 128
WIN = 512
BLK = 64
VB = 6
NSL = 4
MAX_RETRIEVERS = 4


def shifted(block, axis, distance):
    devices = range(lax.axis_size(axis))
    route = [((i - distance) % len(devices), i) for i in devices]
    return lax.ppermute(block, axis, route)


def attend_kernel(roles_ref, slot_ref, count_ref, diag_ref,
                  q_ref, prev_ref, own_ref, vk_ref, vv_ref, sk_ref, sv_ref, o_ref):
    h = pl.program_id(0)
    rows = q_ref.shape[0]
    scaling = 1.0 / math.sqrt(HEAD_SIZE)
    q = q_ref[...]
    dims = (((1,), (1,)), ((), ()))

    def scores(keys):
        return lax.dot_general(q, keys, dims, preferred_element_type=jnp.float32) * scaling

    s_prev = scores(prev_ref[0])
    s_own = scores(own_ref[0])
    row = lax.broadcasted_iota(jnp.int32, (rows, rows), 0)
    col = lax.broadcasted_iota(jnp.int32, (rows, rows), 1)

    def finish(s_side, ok_side, v_side, ok_prev, ok_own):
        neg = -jnp.inf
        m_side = jnp.max(jnp.where(ok_side, s_side, neg), axis=1, keepdims=True)
        m_prev = jnp.max(jnp.where(ok_prev, s_prev, neg), axis=1, keepdims=True)
        m_own = jnp.max(jnp.where(ok_own, s_own, neg), axis=1, keepdims=True)
        m = jnp.maximum(jnp.maximum(m_side, m_prev), m_own)
        e_side = jnp.where(ok_side, jnp.exp(s_side - m), 0.0)
        e_prev = jnp.where(ok_prev, jnp.exp(s_prev - m), 0.0)
        e_own = jnp.where(ok_own, jnp.exp(s_own - m), 0.0)
        total = (jnp.sum(e_side, axis=1, keepdims=True)
                 + jnp.sum(e_prev, axis=1, keepdims=True)
                 + jnp.sum(e_own, axis=1, keepdims=True))
        p_side = (e_side / total).astype(jnp.bfloat16)
        p_prev = (e_prev / total).astype(jnp.bfloat16)
        p_own = (e_own / total).astype(jnp.bfloat16)
        out = jnp.dot(p_side, v_side, preferred_element_type=jnp.float32)
        out = out + jnp.dot(p_prev, prev_ref[1], preferred_element_type=jnp.float32)
        out = out + jnp.dot(p_own, own_ref[1], preferred_element_type=jnp.float32)
        o_ref[...] = out.astype(o_ref.dtype)

    @pl.when(roles_ref[h] != 1)
    def _():
        s_side = scores(sk_ref[...])
        ok_side = jnp.ones(s_side.shape, jnp.bool_)
        finish(s_side, ok_side, sv_ref[...], col > row, col <= row)

    @pl.when(roles_ref[h] == 1)
    def _():
        s_side = scores(vk_ref[...])
        side_col = lax.broadcasted_iota(jnp.int32, s_side.shape, 1)
        ok_side = side_col // BLK < count_ref[h]
        rel_prev = row // BLK + rows // BLK - col // BLK
        rel_own = row // BLK - col // BLK
        ok_prev = jnp.zeros((rows, rows), jnp.bool_)
        ok_own = jnp.zeros((rows, rows), jnp.bool_)
        for d in range(NSL):
            off = diag_ref[h * NSL + d]
            ok_prev = ok_prev | (rel_prev == off)
            ok_own = ok_own | ((rel_own == off) & ((off > 0) | (col <= row)))
        finish(s_side, ok_side, vv_ref[...], ok_prev, ok_own)


def attend(roles_l, slot_l, count_l, diag_l, q_local, prev_kv, own_kv, side):
    rows = q_local.shape[0]
    heads = q_local.shape[1] // HEAD_SIZE
    vrows = VB * BLK
    sink_block = MAX_RETRIEVERS * vrows // SINK
    grid_spec = pltpu.PrefetchScalarGridSpec(
        num_scalar_prefetch=4,
        grid=(heads,),
        in_specs=[
            pl.BlockSpec((rows, HEAD_SIZE), lambda h, *_: (0, h)),
            pl.BlockSpec((2, rows, HEAD_SIZE), lambda h, *_: (0, 0, 0)),
            pl.BlockSpec((2, rows, HEAD_SIZE), lambda h, *_: (0, 0, 0)),
            pl.BlockSpec((None, vrows, HEAD_SIZE), lambda h, r, s, *_: (0, s[h], 0)),
            pl.BlockSpec((None, vrows, HEAD_SIZE), lambda h, r, s, *_: (1, s[h], 0)),
            pl.BlockSpec((None, SINK, HEAD_SIZE), lambda h, *_: (0, sink_block, 0)),
            pl.BlockSpec((None, SINK, HEAD_SIZE), lambda h, *_: (1, sink_block, 0)),
        ],
        out_specs=pl.BlockSpec((rows, HEAD_SIZE), lambda h, *_: (0, h)),
    )
    return pl.pallas_call(
        attend_kernel,
        grid_spec=grid_spec,
        out_shape=jax.ShapeDtypeStruct(q_local.shape, jnp.bfloat16),
    )(roles_l, slot_l, count_l, diag_l, q_local, prev_kv, own_kv, side, side, side, side)


def sum_over_seq(block, seq_devices):
    flat = block.reshape(seq_devices, -1)
    mine = lax.all_to_all(flat, "seq", 0, 0, tiled=True)
    total = jnp.sum(mine.astype(jnp.float32), 0, keepdims=True).astype(block.dtype)
    every = lax.all_to_all(jnp.broadcast_to(total, flat.shape), "seq", 0, 0, tiled=True)
    return every.reshape(block.shape)


def shards(queries, keys, values, prefix_keys, prefix_values, roles, columns, col_count, diagonals):
    seq_devices = lax.axis_size("seq")
    my_seq = lax.axis_index("seq")
    cache_rows = prefix_keys.shape[0]
    blocks_dev = cache_rows // BLK
    heads = roles.shape[0]

    is_ret = roles == 1
    slot = jnp.cumsum(is_ret.astype(jnp.int32)) - 1
    match = is_ret[None, :] & (slot[None, :] == jnp.arange(MAX_RETRIEVERS, dtype=jnp.int32)[:, None])
    head_of_slot = jnp.argmax(match, axis=1)
    cols_s = columns[head_of_slot]
    owner = cols_s // blocks_dev
    local_block = cols_s - owner * blocks_dev
    mine = (owner == my_seq)[:, :, None, None]
    kv_blocks = jnp.stack([prefix_keys, prefix_values], 0).reshape(2, blocks_dev, BLK, HEAD_SIZE)
    pieces = kv_blocks[:, local_block]
    pieces = jnp.where(mine[None], pieces, jnp.zeros_like(pieces))
    pieces = pieces.reshape(2, MAX_RETRIEVERS * VB * BLK, HEAD_SIZE)
    sink = jnp.stack([prefix_keys[:SINK], prefix_values[:SINK]], 0)
    sink = jnp.where(my_seq == 0, sink, jnp.zeros_like(sink))
    side = sum_over_seq(jnp.concatenate([pieces, sink], 1), seq_devices)

    q_local = lax.all_to_all(queries, "head", split_axis=1, concat_axis=0, tiled=True)
    kv = jnp.stack([keys, values], 0)
    kv_local = lax.all_to_all(kv, "head", split_axis=2, concat_axis=1, tiled=True)
    tail_cache = jnp.stack([prefix_keys[cache_rows - WIN:], prefix_values[cache_rows - WIN:]], 0)
    outgoing = jnp.where(my_seq == seq_devices - 1, tail_cache, kv_local)
    prev_kv = shifted(outgoing, "seq", 1)

    slot_l = jnp.where(is_ret, slot, 0).astype(jnp.int32)
    return attend(
        roles.astype(jnp.int32),
        slot_l,
        col_count.astype(jnp.int32),
        diagonals.reshape(heads * NSL).astype(jnp.int32),
        q_local,
        prev_kv,
        kv_local,
        side,
    )


def solution(mesh):
    placed = (
        P(("seq", "head"), None),
        P(("seq", "head"), None),
        P(("seq", "head"), None),
        P("seq", "head"),
        P("seq", "head"),
        P("head"),
        P("head", None),
        P("head"),
        P("head", None),
    )
    return jax.shard_map(
        shards, mesh=mesh, in_specs=placed, out_specs=P("seq", "head"), check_vma=False
    )
```

```python
import functools
import math

import jax
import jax.numpy as jnp
from jax import lax
from jax.experimental import pallas as pl
from jax.experimental.pallas import tpu as pltpu
from jax.sharding import PartitionSpec as P

QUERY_HEADS = 64
KEY_VALUE_HEADS = 8
HEAD_SIZE = 128
SINK = 128
WIN = 512
BLK = 64
VB = 6
NSL = 4
MAX_RETRIEVERS = 4


def shifted(block, axis, distance):
    devices = range(lax.axis_size(axis))
    route = [((i - distance) % len(devices), i) for i in devices]
    return lax.ppermute(block, axis, route)


def attend_kernel(roles_ref, slot_ref, count_ref, diag_ref,
                  q_ref, prev_ref, own_ref, vk_ref, vv_ref, sk_ref, sv_ref, o_ref):
    h = pl.program_id(0)
    rows = q_ref.shape[0]
    scaling = 1.0 / math.sqrt(HEAD_SIZE)
    q = q_ref[...]
    dims = (((1,), (1,)), ((), ()))

    def scores(keys):
        return lax.dot_general(q, keys, dims, preferred_element_type=jnp.float32) * scaling

    s_prev = scores(prev_ref[0])
    s_own = scores(own_ref[0])
    row = lax.broadcasted_iota(jnp.int32, (rows, rows), 0)
    col = lax.broadcasted_iota(jnp.int32, (rows, rows), 1)

    def finish(s_side, ok_side, v_side, ok_prev, ok_own):
        neg = -jnp.inf
        m_side = jnp.max(jnp.where(ok_side, s_side, neg), axis=1, keepdims=True)
        m_prev = jnp.max(jnp.where(ok_prev, s_prev, neg), axis=1, keepdims=True)
        m_own = jnp.max(jnp.where(ok_own, s_own, neg), axis=1, keepdims=True)
        m = jnp.maximum(jnp.maximum(m_side, m_prev), m_own)
        e_side = jnp.where(ok_side, jnp.exp(s_side - m), 0.0)
        e_prev = jnp.where(ok_prev, jnp.exp(s_prev - m), 0.0)
        e_own = jnp.where(ok_own, jnp.exp(s_own - m), 0.0)
        total = (jnp.sum(e_side, axis=1, keepdims=True)
                 + jnp.sum(e_prev, axis=1, keepdims=True)
                 + jnp.sum(e_own, axis=1, keepdims=True))
        p_side = (e_side / total).astype(jnp.bfloat16)
        p_prev = (e_prev / total).astype(jnp.bfloat16)
        p_own = (e_own / total).astype(jnp.bfloat16)
        out = jnp.dot(p_side, v_side, preferred_element_type=jnp.float32)
        out = out + jnp.dot(p_prev, prev_ref[1], preferred_element_type=jnp.float32)
        out = out + jnp.dot(p_own, own_ref[1], preferred_element_type=jnp.float32)
        o_ref[...] = out.astype(o_ref.dtype)

    @pl.when(roles_ref[h] != 1)
    def _():
        s_side = scores(sk_ref[...])
        ok_side = jnp.ones(s_side.shape, jnp.bool_)
        finish(s_side, ok_side, sv_ref[...], col > row, col <= row)

    @pl.when(roles_ref[h] == 1)
    def _():
        s_side = scores(vk_ref[...])
        side_col = lax.broadcasted_iota(jnp.int32, s_side.shape, 1)
        ok_side = side_col // BLK < count_ref[h]
        rel_prev = row // BLK + rows // BLK - col // BLK
        rel_own = row // BLK - col // BLK
        ok_prev = jnp.zeros((rows, rows), jnp.bool_)
        ok_own = jnp.zeros((rows, rows), jnp.bool_)
        for d in range(NSL):
            off = diag_ref[h * NSL + d]
            ok_prev = ok_prev | (rel_prev == off)
            ok_own = ok_own | ((rel_own == off) & ((off > 0) | (col <= row)))
        finish(s_side, ok_side, vv_ref[...], ok_prev, ok_own)


def attend(roles_l, slot_l, count_l, diag_l, q_local, prev_kv, own_kv, side):
    rows = q_local.shape[0]
    heads = q_local.shape[1] // HEAD_SIZE
    vrows = VB * BLK
    sink_block = MAX_RETRIEVERS * vrows // SINK
    grid_spec = pltpu.PrefetchScalarGridSpec(
        num_scalar_prefetch=4,
        grid=(heads,),
        in_specs=[
            pl.BlockSpec((rows, HEAD_SIZE), lambda h, *_: (0, h)),
            pl.BlockSpec((2, rows, HEAD_SIZE), lambda h, *_: (0, 0, 0)),
            pl.BlockSpec((2, rows, HEAD_SIZE), lambda h, *_: (0, 0, 0)),
            pl.BlockSpec((None, vrows, HEAD_SIZE), lambda h, r, s, *_: (0, s[h], 0)),
            pl.BlockSpec((None, vrows, HEAD_SIZE), lambda h, r, s, *_: (1, s[h], 0)),
            pl.BlockSpec((None, SINK, HEAD_SIZE), lambda h, *_: (0, sink_block, 0)),
            pl.BlockSpec((None, SINK, HEAD_SIZE), lambda h, *_: (1, sink_block, 0)),
        ],
        out_specs=pl.BlockSpec((rows, HEAD_SIZE), lambda h, *_: (0, h)),
    )
    return pl.pallas_call(
        attend_kernel,
        grid_spec=grid_spec,
        out_shape=jax.ShapeDtypeStruct(q_local.shape, jnp.bfloat16),
    )(roles_l, slot_l, count_l, diag_l, q_local, prev_kv, own_kv, side, side, side, side)


def sum_over_seq(block, seq_devices):
    flat = block.reshape(seq_devices, -1, block.shape[-1])
    mine = lax.all_to_all(flat, "seq", 0, 0, tiled=True)
    total = jnp.sum(mine.astype(jnp.float32), 0, keepdims=True).astype(block.dtype)
    every = lax.all_to_all(jnp.broadcast_to(total, flat.shape), "seq", 0, 0, tiled=True)
    return every.reshape(block.shape)


def shards(queries, keys, values, prefix_keys, prefix_values, roles, columns, col_count, diagonals):
    seq_devices = lax.axis_size("seq")
    my_seq = lax.axis_index("seq")
    cache_rows = prefix_keys.shape[0]
    blocks_dev = cache_rows // BLK
    heads = roles.shape[0]

    is_ret = roles == 1
    slot = jnp.cumsum(is_ret.astype(jnp.int32)) - 1
    match = is_ret[None, :] & (slot[None, :] == jnp.arange(MAX_RETRIEVERS, dtype=jnp.int32)[:, None])
    head_of_slot = jnp.argmax(match, axis=1)
    cols_s = columns[head_of_slot]
    owner = cols_s // blocks_dev
    local_block = cols_s - owner * blocks_dev
    mine = (owner == my_seq)[:, :, None, None]
    kv_blocks = jnp.stack([prefix_keys, prefix_values], 0).reshape(2, blocks_dev, BLK, HEAD_SIZE)
    pieces = kv_blocks[:, local_block]
    pieces = jnp.where(mine[None], pieces, jnp.zeros_like(pieces))
    pieces = pieces.reshape(2, MAX_RETRIEVERS * VB * BLK, HEAD_SIZE)
    sink = jnp.stack([prefix_keys[:SINK], prefix_values[:SINK]], 0)
    sink = jnp.where(my_seq == 0, sink, jnp.zeros_like(sink))
    both = jnp.concatenate([pieces, sink], 1)

    kv = jnp.stack([keys, values], 0)
    kv_local = lax.all_to_all(kv, "head", split_axis=2, concat_axis=1, tiled=True)
    tail_cache = jnp.stack([prefix_keys[cache_rows - WIN:], prefix_values[cache_rows - WIN:]], 0)
    outgoing = jnp.where(my_seq == seq_devices - 1, tail_cache, kv_local)
    prev_kv = shifted(outgoing, "seq", 1)
    both, kv_local = lax.optimization_barrier((both, kv_local))
    side = sum_over_seq(both, seq_devices)
    q_local = lax.all_to_all(queries, "head", split_axis=1, concat_axis=0, tiled=True)

    slot_l = jnp.where(is_ret, slot, 0).astype(jnp.int32)
    return attend(
        roles.astype(jnp.int32),
        slot_l,
        col_count.astype(jnp.int32),
        diagonals.reshape(heads * NSL).astype(jnp.int32),
        q_local,
        prev_kv,
        kv_local,
        side,
    )


def solution(mesh):
    placed = (
        P(("seq", "head"), None),
        P(("seq", "head"), None),
        P(("seq", "head"), None),
        P("seq", "head"),
        P("seq", "head"),
        P("head"),
        P("head", None),
        P("head"),
        P("head", None),
    )
    return jax.shard_map(
        shards, mesh=mesh, in_specs=placed, out_specs=P("seq", "head"), check_vma=False
    )
```

```python
import functools
import math

import jax
import jax.numpy as jnp
from jax import lax
from jax.experimental import pallas as pl
from jax.experimental.pallas import tpu as pltpu
from jax.sharding import PartitionSpec as P

QUERY_HEADS = 64
KEY_VALUE_HEADS = 8
HEAD_SIZE = 128
SINK = 128
WIN = 512
BLK = 64
VB = 6
NSL = 4
MAX_RETRIEVERS = 4


def shifted(block, axis, distance):
    devices = range(lax.axis_size(axis))
    route = [((i - distance) % len(devices), i) for i in devices]
    return lax.ppermute(block, axis, route)


def attend_kernel(roles_ref, slot_ref, count_ref, diag_ref,
                  q_ref, prev_ref, own_ref, vk_ref, vv_ref, sk_ref, sv_ref, o_ref):
    h = pl.program_id(0)
    rows = q_ref.shape[0]
    scaling = 1.0 / math.sqrt(HEAD_SIZE)
    q = q_ref[...]
    dims = (((1,), (1,)), ((), ()))

    def scores(keys):
        return lax.dot_general(q, keys, dims, preferred_element_type=jnp.float32) * scaling

    s_prev = scores(prev_ref[0])
    s_own = scores(own_ref[0])
    row = lax.broadcasted_iota(jnp.int32, (rows, rows), 0)
    col = lax.broadcasted_iota(jnp.int32, (rows, rows), 1)

    def finish(s_side, ok_side, v_side, ok_prev, ok_own):
        neg = -jnp.inf
        m_side = jnp.max(jnp.where(ok_side, s_side, neg), axis=1, keepdims=True)
        m_prev = jnp.max(jnp.where(ok_prev, s_prev, neg), axis=1, keepdims=True)
        m_own = jnp.max(jnp.where(ok_own, s_own, neg), axis=1, keepdims=True)
        m = jnp.maximum(jnp.maximum(m_side, m_prev), m_own)
        e_side = jnp.where(ok_side, jnp.exp(s_side - m), 0.0)
        e_prev = jnp.where(ok_prev, jnp.exp(s_prev - m), 0.0)
        e_own = jnp.where(ok_own, jnp.exp(s_own - m), 0.0)
        total = (jnp.sum(e_side, axis=1, keepdims=True)
                 + jnp.sum(e_prev, axis=1, keepdims=True)
                 + jnp.sum(e_own, axis=1, keepdims=True))
        p_side = (e_side / total).astype(jnp.bfloat16)
        p_prev = (e_prev / total).astype(jnp.bfloat16)
        p_own = (e_own / total).astype(jnp.bfloat16)
        out = jnp.dot(p_side, v_side, preferred_element_type=jnp.float32)
        out = out + jnp.dot(p_prev, prev_ref[1], preferred_element_type=jnp.float32)
        out = out + jnp.dot(p_own, own_ref[1], preferred_element_type=jnp.float32)
        o_ref[...] = out.astype(o_ref.dtype)

    @pl.when(roles_ref[h] != 1)
    def _():
        s_side = scores(sk_ref[...])
        ok_side = jnp.ones(s_side.shape, jnp.bool_)
        finish(s_side, ok_side, sv_ref[...], col > row, col <= row)

    @pl.when(roles_ref[h] == 1)
    def _():
        s_side = scores(vk_ref[...])
        side_col = lax.broadcasted_iota(jnp.int32, s_side.shape, 1)
        ok_side = side_col // BLK < count_ref[h]
        rel_prev = row // BLK + rows // BLK - col // BLK
        rel_own = row // BLK - col // BLK
        ok_prev = jnp.zeros((rows, rows), jnp.bool_)
        ok_own = jnp.zeros((rows, rows), jnp.bool_)
        for d in range(NSL):
            off = diag_ref[h * NSL + d]
            ok_prev = ok_prev | (rel_prev == off)
            ok_own = ok_own | ((rel_own == off) & ((off > 0) | (col <= row)))
        finish(s_side, ok_side, vv_ref[...], ok_prev, ok_own)


def attend(roles_l, slot_l, count_l, diag_l, q_local, prev_kv, own_kv, side):
    rows = q_local.shape[0]
    heads = q_local.shape[1] // HEAD_SIZE
    vrows = VB * BLK
    sink_block = MAX_RETRIEVERS * vrows // SINK
    grid_spec = pltpu.PrefetchScalarGridSpec(
        num_scalar_prefetch=4,
        grid=(heads,),
        in_specs=[
            pl.BlockSpec((rows, HEAD_SIZE), lambda h, *_: (0, h)),
            pl.BlockSpec((2, rows, HEAD_SIZE), lambda h, *_: (0, 0, 0)),
            pl.BlockSpec((2, rows, HEAD_SIZE), lambda h, *_: (0, 0, 0)),
            pl.BlockSpec((None, vrows, HEAD_SIZE), lambda h, r, s, *_: (0, s[h], 0)),
            pl.BlockSpec((None, vrows, HEAD_SIZE), lambda h, r, s, *_: (1, s[h], 0)),
            pl.BlockSpec((None, SINK, HEAD_SIZE), lambda h, *_: (0, sink_block, 0)),
            pl.BlockSpec((None, SINK, HEAD_SIZE), lambda h, *_: (1, sink_block, 0)),
        ],
        out_specs=pl.BlockSpec((rows, HEAD_SIZE), lambda h, *_: (0, h)),
    )
    return pl.pallas_call(
        attend_kernel,
        grid_spec=grid_spec,
        out_shape=jax.ShapeDtypeStruct(q_local.shape, jnp.bfloat16),
    )(roles_l, slot_l, count_l, diag_l, q_local, prev_kv, own_kv, side, side, side, side)


def scatter_sum(block, seq_devices):
    flat = block.reshape(seq_devices, -1, block.shape[-1])
    mine = lax.all_to_all(flat, "seq", 0, 0, tiled=True)
    return jnp.sum(mine.astype(jnp.float32), 0, keepdims=True).astype(block.dtype)


def gather_sums(total, shape, seq_devices):
    every = lax.all_to_all(jnp.broadcast_to(total, (seq_devices,) + total.shape[1:]), "seq", 0, 0, tiled=True)
    return every.reshape(shape)


def shards(queries, keys, values, prefix_keys, prefix_values, roles, columns, col_count, diagonals):
    seq_devices = lax.axis_size("seq")
    my_seq = lax.axis_index("seq")
    cache_rows = prefix_keys.shape[0]
    blocks_dev = cache_rows // BLK
    heads = roles.shape[0]

    is_ret = roles == 1
    slot = jnp.cumsum(is_ret.astype(jnp.int32)) - 1
    match = is_ret[None, :] & (slot[None, :] == jnp.arange(MAX_RETRIEVERS, dtype=jnp.int32)[:, None])
    head_of_slot = jnp.argmax(match, axis=1)
    cols_s = columns[head_of_slot]
    owner = cols_s // blocks_dev
    local_block = cols_s - owner * blocks_dev
    mine = (owner == my_seq)[:, :, None, None]
    kv_blocks = jnp.stack([prefix_keys, prefix_values], 0).reshape(2, blocks_dev, BLK, HEAD_SIZE)
    pieces = kv_blocks[:, local_block]
    pieces = jnp.where(mine[None], pieces, jnp.zeros_like(pieces))
    pieces = pieces.reshape(2, MAX_RETRIEVERS * VB * BLK, HEAD_SIZE)
    sink = jnp.stack([prefix_keys[:SINK], prefix_values[:SINK]], 0)
    sink = jnp.where(my_seq == 0, sink, jnp.zeros_like(sink))
    both = jnp.concatenate([pieces, sink], 1)

    kv = jnp.stack([keys, values], 0)
    kv_local = lax.all_to_all(kv, "head", split_axis=2, concat_axis=1, tiled=True)
    tail_cache = jnp.stack([prefix_keys[cache_rows - WIN:], prefix_values[cache_rows - WIN:]], 0)
    outgoing = jnp.where(my_seq == seq_devices - 1, tail_cache, kv_local)
    prev_kv = shifted(outgoing, "seq", 1)
    q_local = lax.all_to_all(queries, "head", split_axis=1, concat_axis=0, tiled=True)
    total = scatter_sum(both, seq_devices)
    total, prev_kv, q_local = lax.optimization_barrier((total, prev_kv, q_local))
    side = gather_sums(total, both.shape, seq_devices)

    slot_l = jnp.where(is_ret, slot, 0).astype(jnp.int32)
    return attend(
        roles.astype(jnp.int32),
        slot_l,
        col_count.astype(jnp.int32),
        diagonals.reshape(heads * NSL).astype(jnp.int32),
        q_local,
        prev_kv,
        kv_local,
        side,
    )


def solution(mesh):
    placed = (
        P(("seq", "head"), None),
        P(("seq", "head"), None),
        P(("seq", "head"), None),
        P("seq", "head"),
        P("seq", "head"),
        P("head"),
        P("head", None),
        P("head"),
        P("head", None),
    )
    return jax.shard_map(
        shards, mesh=mesh, in_specs=placed, out_specs=P("seq", "head"), check_vma=False
    )
```

```python
import functools
import math

import jax
import jax.numpy as jnp
from jax import lax
from jax.experimental import pallas as pl
from jax.experimental.pallas import tpu as pltpu
from jax.sharding import PartitionSpec as P

QUERY_HEADS = 64
KEY_VALUE_HEADS = 8
HEAD_SIZE = 128
SINK = 128
WIN = 512
BLK = 64
VB = 6
NSL = 4
MAX_RETRIEVERS = 4


def shifted(block, axis, distance):
    devices = range(lax.axis_size(axis))
    route = [((i - distance) % len(devices), i) for i in devices]
    return lax.ppermute(block, axis, route)


def attend_kernel(roles_ref, slot_ref, count_ref, diag_ref,
                  q_ref, prev_ref, own_ref, vk_ref, vv_ref, sk_ref, sv_ref, o_ref):
    h = pl.program_id(0)
    rows = q_ref.shape[0]
    scaling = 1.0 / math.sqrt(HEAD_SIZE)
    q = q_ref[...]
    dims = (((1,), (1,)), ((), ()))

    def scores(keys):
        return lax.dot_general(q, keys, dims, preferred_element_type=jnp.float32) * scaling

    s_prev = scores(prev_ref[0])
    s_own = scores(own_ref[0])
    row = lax.broadcasted_iota(jnp.int32, (rows, rows), 0)
    col = lax.broadcasted_iota(jnp.int32, (rows, rows), 1)

    def finish(s_side, ok_side, v_side, ok_prev, ok_own):
        neg = -jnp.inf
        m_side = jnp.max(jnp.where(ok_side, s_side, neg), axis=1, keepdims=True)
        m_prev = jnp.max(jnp.where(ok_prev, s_prev, neg), axis=1, keepdims=True)
        m_own = jnp.max(jnp.where(ok_own, s_own, neg), axis=1, keepdims=True)
        m = jnp.maximum(jnp.maximum(m_side, m_prev), m_own)
        e_side = jnp.where(ok_side, jnp.exp(s_side - m), 0.0)
        e_prev = jnp.where(ok_prev, jnp.exp(s_prev - m), 0.0)
        e_own = jnp.where(ok_own, jnp.exp(s_own - m), 0.0)
        total = (jnp.sum(e_side, axis=1, keepdims=True)
                 + jnp.sum(e_prev, axis=1, keepdims=True)
                 + jnp.sum(e_own, axis=1, keepdims=True))
        p_side = (e_side / total).astype(jnp.bfloat16)
        p_prev = (e_prev / total).astype(jnp.bfloat16)
        p_own = (e_own / total).astype(jnp.bfloat16)
        out = jnp.dot(p_side, v_side, preferred_element_type=jnp.float32)
        out = out + jnp.dot(p_prev, prev_ref[1], preferred_element_type=jnp.float32)
        out = out + jnp.dot(p_own, own_ref[1], preferred_element_type=jnp.float32)
        o_ref[...] = out.astype(o_ref.dtype)

    @pl.when(roles_ref[h] != 1)
    def _():
        s_side = scores(sk_ref[...])
        ok_side = jnp.ones(s_side.shape, jnp.bool_)
        finish(s_side, ok_side, sv_ref[...], col > row, col <= row)

    @pl.when(roles_ref[h] == 1)
    def _():
        s_side = scores(vk_ref[...])
        side_col = lax.broadcasted_iota(jnp.int32, s_side.shape, 1)
        ok_side = side_col // BLK < count_ref[h]
        rel_prev = row // BLK + rows // BLK - col // BLK
        rel_own = row // BLK - col // BLK
        ok_prev = jnp.zeros((rows, rows), jnp.bool_)
        ok_own = jnp.zeros((rows, rows), jnp.bool_)
        for d in range(NSL):
            off = diag_ref[h * NSL + d]
            ok_prev = ok_prev | (rel_prev == off)
            ok_own = ok_own | ((rel_own == off) & ((off > 0) | (col <= row)))
        finish(s_side, ok_side, vv_ref[...], ok_prev, ok_own)


def attend(roles_l, slot_l, count_l, diag_l, q_local, prev_kv, own_kv, side):
    rows = q_local.shape[0]
    heads = q_local.shape[1] // HEAD_SIZE
    vrows = VB * BLK
    sink_block = MAX_RETRIEVERS * vrows // SINK
    grid_spec = pltpu.PrefetchScalarGridSpec(
        num_scalar_prefetch=4,
        grid=(heads,),
        in_specs=[
            pl.BlockSpec((rows, HEAD_SIZE), lambda h, *_: (0, h)),
            pl.BlockSpec((2, rows, HEAD_SIZE), lambda h, *_: (0, 0, 0)),
            pl.BlockSpec((2, rows, HEAD_SIZE), lambda h, *_: (0, 0, 0)),
            pl.BlockSpec((None, vrows, HEAD_SIZE), lambda h, r, s, *_: (0, s[h], 0)),
            pl.BlockSpec((None, vrows, HEAD_SIZE), lambda h, r, s, *_: (1, s[h], 0)),
            pl.BlockSpec((None, SINK, HEAD_SIZE), lambda h, *_: (0, sink_block, 0)),
            pl.BlockSpec((None, SINK, HEAD_SIZE), lambda h, *_: (1, sink_block, 0)),
        ],
        out_specs=pl.BlockSpec((rows, HEAD_SIZE), lambda h, *_: (0, h)),
    )
    return pl.pallas_call(
        attend_kernel,
        grid_spec=grid_spec,
        out_shape=jax.ShapeDtypeStruct(q_local.shape, jnp.bfloat16),
    )(roles_l, slot_l, count_l, diag_l, q_local, prev_kv, own_kv, side, side, side, side)


def scatter_sum(block, seq_devices):
    flat = block.reshape(seq_devices, -1, block.shape[-1])
    mine = lax.all_to_all(flat, "seq", 0, 0, tiled=True)
    return jnp.sum(mine.astype(jnp.float32), 0, keepdims=True).astype(block.dtype)


def gather_sums(total, shape, seq_devices):
    every = lax.all_to_all(jnp.broadcast_to(total, (seq_devices,) + total.shape[1:]), "seq", 0, 0, tiled=True)
    return every.reshape(shape)


def shards(queries, keys, values, prefix_keys, prefix_values, roles, columns, col_count, diagonals):
    seq_devices = lax.axis_size("seq")
    my_seq = lax.axis_index("seq")
    cache_rows = prefix_keys.shape[0]
    blocks_dev = cache_rows // BLK
    heads = roles.shape[0]

    is_ret = roles == 1
    slot = jnp.cumsum(is_ret.astype(jnp.int32)) - 1
    match = is_ret[None, :] & (slot[None, :] == jnp.arange(MAX_RETRIEVERS, dtype=jnp.int32)[:, None])
    head_of_slot = jnp.argmax(match, axis=1)
    cols_s = columns[head_of_slot]
    owner = cols_s // blocks_dev
    local_block = cols_s - owner * blocks_dev
    mine = (owner == my_seq)[:, :, None, None]
    kv_blocks = jnp.stack([prefix_keys, prefix_values], 0).reshape(2, blocks_dev, BLK, HEAD_SIZE)
    pieces = kv_blocks[:, local_block]
    pieces = jnp.where(mine[None], pieces, jnp.zeros_like(pieces))
    pieces = pieces.reshape(2, MAX_RETRIEVERS * VB * BLK, HEAD_SIZE)
    sink = jnp.stack([prefix_keys[:SINK], prefix_values[:SINK]], 0)
    sink = jnp.where(my_seq == 0, sink, jnp.zeros_like(sink))
    both = jnp.concatenate([pieces, sink], 1)

    kv = jnp.stack([keys, values], 0)
    kv_local = lax.all_to_all(kv, "head", split_axis=2, concat_axis=1, tiled=True)
    tail_cache = jnp.stack([prefix_keys[cache_rows - WIN:], prefix_values[cache_rows - WIN:]], 0)
    outgoing = jnp.where(my_seq == seq_devices - 1, tail_cache, kv_local)
    q_local = lax.all_to_all(queries, "head", split_axis=1, concat_axis=0, tiled=True)
    both, q_local = lax.optimization_barrier((both, q_local))
    total = scatter_sum(both, seq_devices)
    total, outgoing = lax.optimization_barrier((total, outgoing))
    prev_kv = shifted(outgoing, "seq", 1)
    side = gather_sums(total, both.shape, seq_devices)

    slot_l = jnp.where(is_ret, slot, 0).astype(jnp.int32)
    return attend(
        roles.astype(jnp.int32),
        slot_l,
        col_count.astype(jnp.int32),
        diagonals.reshape(heads * NSL).astype(jnp.int32),
        q_local,
        prev_kv,
        kv_local,
        side,
    )


def solution(mesh):
    placed = (
        P(("seq", "head"), None),
        P(("seq", "head"), None),
        P(("seq", "head"), None),
        P("seq", "head"),
        P("seq", "head"),
        P("head"),
        P("head", None),
        P("head"),
        P("head", None),
    )
    return jax.shard_map(
        shards, mesh=mesh, in_specs=placed, out_specs=P("seq", "head"), check_vma=False
    )
```

```python
import functools
import math

import jax
import jax.numpy as jnp
from jax import lax
from jax.experimental import pallas as pl
from jax.experimental.pallas import tpu as pltpu
from jax.sharding import PartitionSpec as P

QUERY_HEADS = 64
KEY_VALUE_HEADS = 8
HEAD_SIZE = 128
SINK = 128
WIN = 512
BLK = 64
VB = 6
NSL = 4
MAX_RETRIEVERS = 4


def shifted(block, axis, distance):
    devices = range(lax.axis_size(axis))
    route = [((i - distance) % len(devices), i) for i in devices]
    return lax.ppermute(block, axis, route)


def attend_kernel(roles_ref, slot_ref, count_ref, diag_ref,
                  q_ref, ck_ref, cv_ref, vk_ref, vv_ref, sk_ref, sv_ref, o_ref):
    h = pl.program_id(0)
    rows = q_ref.shape[0]
    back = ck_ref.shape[0] - rows
    scaling = 1.0 / math.sqrt(HEAD_SIZE)
    dims = (((1,), (1,)), ((), ()))
    neg = -jnp.inf

    def scores(q, keys):
        return lax.dot_general(q, keys, dims, preferred_element_type=jnp.float32) * scaling

    def softmax_out(s_a, ok_a, v_a, s_b, ok_b, v_b):
        m = jnp.maximum(jnp.max(jnp.where(ok_a, s_a, neg), axis=1, keepdims=True),
                        jnp.max(jnp.where(ok_b, s_b, neg), axis=1, keepdims=True))
        e_a = jnp.where(ok_a, jnp.exp(s_a - m), 0.0)
        e_b = jnp.where(ok_b, jnp.exp(s_b - m), 0.0)
        total = jnp.sum(e_a, axis=1, keepdims=True) + jnp.sum(e_b, axis=1, keepdims=True)
        out = jnp.dot((e_a / total).astype(jnp.bfloat16), v_a, preferred_element_type=jnp.float32)
        out = out + jnp.dot((e_b / total).astype(jnp.bfloat16), v_b, preferred_element_type=jnp.float32)
        return out.astype(o_ref.dtype)

    @pl.when(roles_ref[h] != 1)
    def _():
        sk = sk_ref[...]
        sv = sv_ref[...]
        span = WIN + BLK
        r = lax.broadcasted_iota(jnp.int32, (BLK, span), 0)
        c = lax.broadcasted_iota(jnp.int32, (BLK, span), 1)
        ok_win = (c > r) & (c <= r + WIN)
        ok_sink = jnp.ones((BLK, sk.shape[0]), jnp.bool_)
        for qb in range(rows // BLK):
            lo = qb * BLK + back - WIN
            qv = q_ref[qb * BLK:(qb + 1) * BLK, :]
            s_sink = scores(qv, sk)
            s_win = scores(qv, ck_ref[lo:lo + span, :])
            o_ref[qb * BLK:(qb + 1) * BLK, :] = softmax_out(
                s_sink, ok_sink, sv, s_win, ok_win, cv_ref[lo:lo + span, :])

    @pl.when(roles_ref[h] == 1)
    def _():
        vk = vk_ref[...]
        vv = vv_ref[...]
        cv_ = lax.broadcasted_iota(jnp.int32, (BLK, vk.shape[0]), 1)
        ok_vert = cv_ // BLK < count_ref[h]
        r = lax.broadcasted_iota(jnp.int32, (BLK, NSL * BLK), 0)
        c = lax.broadcasted_iota(jnp.int32, (BLK, NSL * BLK), 1)
        offs = [jnp.clip(diag_ref[h * NSL + d], 0, WIN // BLK - 1) for d in range(NSL)]
        off_col = jnp.zeros((BLK, NSL * BLK), jnp.int32)
        for d in range(NSL):
            off_col = jnp.where(c // BLK == d, offs[d], off_col)
        ok_slash = (off_col > 0) | (c % BLK <= r)
        for qb in range(rows // BLK):
            qv = q_ref[qb * BLK:(qb + 1) * BLK, :]
            s_vert = scores(qv, vk)
            starts = [pl.multiple_of((back // BLK + qb - offs[d]) * BLK, BLK) for d in range(NSL)]
            keys = jnp.concatenate([ck_ref[pl.ds(st, BLK), :] for st in starts], 0)
            vals = jnp.concatenate([cv_ref[pl.ds(st, BLK), :] for st in starts], 0)
            s_slash = scores(qv, keys)
            o_ref[qb * BLK:(qb + 1) * BLK, :] = softmax_out(
                s_vert, ok_vert, vv, s_slash, ok_slash, vals)


def attend(roles_l, slot_l, count_l, diag_l, q_local, comb, side):
    rows = q_local.shape[0]
    heads = q_local.shape[1] // HEAD_SIZE
    crows = comb.shape[1]
    vrows = VB * BLK
    sink_block = MAX_RETRIEVERS * vrows // SINK
    grid_spec = pltpu.PrefetchScalarGridSpec(
        num_scalar_prefetch=4,
        grid=(heads,),
        in_specs=[
            pl.BlockSpec((rows, HEAD_SIZE), lambda h, *_: (0, h)),
            pl.BlockSpec((None, crows, HEAD_SIZE), lambda h, *_: (0, 0, 0)),
            pl.BlockSpec((None, crows, HEAD_SIZE), lambda h, *_: (1, 0, 0)),
            pl.BlockSpec((None, vrows, HEAD_SIZE), lambda h, r, s, *_: (0, s[h], 0)),
            pl.BlockSpec((None, vrows, HEAD_SIZE), lambda h, r, s, *_: (1, s[h], 0)),
            pl.BlockSpec((None, SINK, HEAD_SIZE), lambda h, *_: (0, sink_block, 0)),
            pl.BlockSpec((None, SINK, HEAD_SIZE), lambda h, *_: (1, sink_block, 0)),
        ],
        out_specs=pl.BlockSpec((rows, HEAD_SIZE), lambda h, *_: (0, h)),
    )
    return pl.pallas_call(
        attend_kernel,
        grid_spec=grid_spec,
        out_shape=jax.ShapeDtypeStruct(q_local.shape, jnp.bfloat16),
    )(roles_l, slot_l, count_l, diag_l, q_local, comb, comb, side, side, side, side)


def scatter_sum(block, seq_devices):
    flat = block.reshape(seq_devices, -1, block.shape[-1])
    mine = lax.all_to_all(flat, "seq", 0, 0, tiled=True)
    return jnp.sum(mine.astype(jnp.float32), 0, keepdims=True).astype(block.dtype)


def gather_sums(total, shape, seq_devices):
    every = lax.all_to_all(jnp.broadcast_to(total, (seq_devices,) + total.shape[1:]), "seq", 0, 0, tiled=True)
    return every.reshape(shape)


def shards(queries, keys, values, prefix_keys, prefix_values, roles, columns, col_count, diagonals):
    seq_devices = lax.axis_size("seq")
    my_seq = lax.axis_index("seq")
    cache_rows = prefix_keys.shape[0]
    blocks_dev = cache_rows // BLK
    heads = roles.shape[0]

    is_ret = roles == 1
    slot = jnp.cumsum(is_ret.astype(jnp.int32)) - 1
    match = is_ret[None, :] & (slot[None, :] == jnp.arange(MAX_RETRIEVERS, dtype=jnp.int32)[:, None])
    head_of_slot = jnp.argmax(match, axis=1)
    cols_s = columns[head_of_slot]
    owner = cols_s // blocks_dev
    local_block = cols_s - owner * blocks_dev
    mine = (owner == my_seq)[:, :, None, None]
    kv_blocks = jnp.stack([prefix_keys, prefix_values], 0).reshape(2, blocks_dev, BLK, HEAD_SIZE)
    pieces = kv_blocks[:, local_block]
    pieces = jnp.where(mine[None], pieces, jnp.zeros_like(pieces))
    pieces = pieces.reshape(2, MAX_RETRIEVERS * VB * BLK, HEAD_SIZE)
    sink = jnp.stack([prefix_keys[:SINK], prefix_values[:SINK]], 0)
    sink = jnp.where(my_seq == 0, sink, jnp.zeros_like(sink))
    both = jnp.concatenate([pieces, sink], 1)

    kv = jnp.stack([keys, values], 0)
    kv_local = lax.all_to_all(kv, "head", split_axis=2, concat_axis=1, tiled=True)
    tail_cache = jnp.stack([prefix_keys[cache_rows - WIN:], prefix_values[cache_rows - WIN:]], 0)
    outgoing = jnp.where(my_seq == seq_devices - 1, tail_cache, kv_local)
    q_local = lax.all_to_all(queries, "head", split_axis=1, concat_axis=0, tiled=True)
    both, q_local = lax.optimization_barrier((both, q_local))
    total = scatter_sum(both, seq_devices)
    total, outgoing = lax.optimization_barrier((total, outgoing))
    prev_kv = shifted(outgoing, "seq", 1)
    side = gather_sums(total, both.shape, seq_devices)

    slot_l = jnp.where(is_ret, slot, 0).astype(jnp.int32)
    return attend(
        roles.astype(jnp.int32),
        slot_l,
        col_count.astype(jnp.int32),
        diagonals.reshape(heads * NSL).astype(jnp.int32),
        q_local,
        jnp.concatenate([prev_kv, kv_local], 1),
        side,
    )


def solution(mesh):
    placed = (
        P(("seq", "head"), None),
        P(("seq", "head"), None),
        P(("seq", "head"), None),
        P("seq", "head"),
        P("seq", "head"),
        P("head"),
        P("head", None),
        P("head"),
        P("head", None),
    )
    return jax.shard_map(
        shards, mesh=mesh, in_specs=placed, out_specs=P("seq", "head"), check_vma=False
    )
```

```python
import functools
import math

import jax
import jax.numpy as jnp
from jax import lax
from jax.experimental import pallas as pl
from jax.experimental.pallas import tpu as pltpu
from jax.sharding import PartitionSpec as P

QUERY_HEADS = 64
KEY_VALUE_HEADS = 8
HEAD_SIZE = 128
SINK = 128
WIN = 512
BLK = 64
VB = 6
NSL = 4
MAX_RETRIEVERS = 4


def shifted(block, axis, distance):
    devices = range(lax.axis_size(axis))
    route = [((i - distance) % len(devices), i) for i in devices]
    return lax.ppermute(block, axis, route)


def attend_kernel(roles_ref, slot_ref, count_ref, diag_ref,
                  q_ref, prev_ref, own_ref, vk_ref, vv_ref, sk_ref, sv_ref, o_ref):
    h = pl.program_id(0)
    rows = q_ref.shape[0]
    scaling = 1.0 / math.sqrt(HEAD_SIZE)
    q = q_ref[...]
    dims = (((1,), (1,)), ((), ()))

    def scores(keys):
        return lax.dot_general(q, keys, dims, preferred_element_type=jnp.float32) * scaling

    s_prev = scores(prev_ref[0])
    s_own = scores(own_ref[0])
    row = lax.broadcasted_iota(jnp.int32, (rows, rows), 0)
    col = lax.broadcasted_iota(jnp.int32, (rows, rows), 1)

    def finish(s_side, ok_side, v_side, ok_prev, ok_own):
        neg = -jnp.inf
        m_side = jnp.max(jnp.where(ok_side, s_side, neg), axis=1, keepdims=True)
        m_prev = jnp.max(jnp.where(ok_prev, s_prev, neg), axis=1, keepdims=True)
        m_own = jnp.max(jnp.where(ok_own, s_own, neg), axis=1, keepdims=True)
        m = jnp.maximum(jnp.maximum(m_side, m_prev), m_own)
        e_side = jnp.where(ok_side, jnp.exp(s_side - m), 0.0)
        e_prev = jnp.where(ok_prev, jnp.exp(s_prev - m), 0.0)
        e_own = jnp.where(ok_own, jnp.exp(s_own - m), 0.0)
        total = (jnp.sum(e_side, axis=1, keepdims=True)
                 + jnp.sum(e_prev, axis=1, keepdims=True)
                 + jnp.sum(e_own, axis=1, keepdims=True))
        p_side = (e_side / total).astype(jnp.bfloat16)
        p_prev = (e_prev / total).astype(jnp.bfloat16)
        p_own = (e_own / total).astype(jnp.bfloat16)
        out = jnp.dot(p_side, v_side, preferred_element_type=jnp.float32)
        out = out + jnp.dot(p_prev, prev_ref[1], preferred_element_type=jnp.float32)
        out = out + jnp.dot(p_own, own_ref[1], preferred_element_type=jnp.float32)
        o_ref[...] = out.astype(o_ref.dtype)

    @pl.when(roles_ref[h] != 1)
    def _():
        s_side = scores(sk_ref[...])
        ok_side = jnp.ones(s_side.shape, jnp.bool_)
        finish(s_side, ok_side, sv_ref[...], col > row, col <= row)

    @pl.when(roles_ref[h] == 1)
    def _():
        s_side = scores(vk_ref[...])
        side_col = lax.broadcasted_iota(jnp.int32, s_side.shape, 1)
        ok_side = side_col // BLK < count_ref[h]
        rel_prev = row // BLK + rows // BLK - col // BLK
        rel_own = row // BLK - col // BLK
        ok_prev = jnp.zeros((rows, rows), jnp.bool_)
        ok_own = jnp.zeros((rows, rows), jnp.bool_)
        for d in range(NSL):
            off = diag_ref[h * NSL + d]
            ok_prev = ok_prev | (rel_prev == off)
            ok_own = ok_own | ((rel_own == off) & ((off > 0) | (col <= row)))
        finish(s_side, ok_side, vv_ref[...], ok_prev, ok_own)


def attend(roles_l, slot_l, count_l, diag_l, q_local, prev_kv, own_kv, side):
    rows = q_local.shape[0]
    heads = q_local.shape[1] // HEAD_SIZE
    vrows = VB * BLK
    sink_block = MAX_RETRIEVERS * vrows // SINK
    grid_spec = pltpu.PrefetchScalarGridSpec(
        num_scalar_prefetch=4,
        grid=(heads,),
        in_specs=[
            pl.BlockSpec((rows, HEAD_SIZE), lambda h, *_: (0, h)),
            pl.BlockSpec((2, rows, HEAD_SIZE), lambda h, *_: (0, 0, 0)),
            pl.BlockSpec((2, rows, HEAD_SIZE), lambda h, *_: (0, 0, 0)),
            pl.BlockSpec((None, vrows, HEAD_SIZE), lambda h, r, s, *_: (0, s[h], 0)),
            pl.BlockSpec((None, vrows, HEAD_SIZE), lambda h, r, s, *_: (1, s[h], 0)),
            pl.BlockSpec((None, SINK, HEAD_SIZE), lambda h, *_: (0, sink_block, 0)),
            pl.BlockSpec((None, SINK, HEAD_SIZE), lambda h, *_: (1, sink_block, 0)),
        ],
        out_specs=pl.BlockSpec((rows, HEAD_SIZE), lambda h, *_: (0, h)),
    )
    return pl.pallas_call(
        attend_kernel,
        grid_spec=grid_spec,
        out_shape=jax.ShapeDtypeStruct(q_local.shape, jnp.bfloat16),
    )(roles_l, slot_l, count_l, diag_l, q_local, prev_kv, own_kv, side, side, side, side)


def scatter_sum(block, seq_devices):
    flat = block.reshape(seq_devices, -1, block.shape[-1])
    mine = lax.all_to_all(flat, "seq", 0, 0, tiled=True)
    return jnp.sum(mine.astype(jnp.float32), 0, keepdims=True).astype(block.dtype)


def gather_sums(total, shape, seq_devices):
    every = lax.all_to_all(jnp.broadcast_to(total, (seq_devices,) + total.shape[1:]), "seq", 0, 0, tiled=True)
    return every.reshape(shape)


def shards(queries, keys, values, prefix_keys, prefix_values, roles, columns, col_count, diagonals):
    seq_devices = lax.axis_size("seq")
    my_seq = lax.axis_index("seq")
    cache_rows = prefix_keys.shape[0]
    blocks_dev = cache_rows // BLK
    heads = roles.shape[0]

    is_ret = roles == 1
    slot = jnp.cumsum(is_ret.astype(jnp.int32)) - 1
    match = is_ret[None, :] & (slot[None, :] == jnp.arange(MAX_RETRIEVERS, dtype=jnp.int32)[:, None])
    head_of_slot = jnp.argmax(match, axis=1)
    cols_s = columns[head_of_slot]
    owner = cols_s // blocks_dev
    local_block = cols_s - owner * blocks_dev
    mine = (owner == my_seq)[:, :, None, None]
    kv_blocks = jnp.stack([prefix_keys, prefix_values], 0).reshape(2, blocks_dev, BLK, HEAD_SIZE)
    pieces = kv_blocks[:, local_block]
    pieces = jnp.where(mine[None], pieces, jnp.zeros_like(pieces))
    pieces = pieces.reshape(2, MAX_RETRIEVERS * VB * BLK, HEAD_SIZE)
    sink = jnp.stack([prefix_keys[:SINK], prefix_values[:SINK]], 0)
    sink = jnp.where(my_seq == 0, sink, jnp.zeros_like(sink))
    both = jnp.concatenate([pieces, sink], 1)

    head_devices = lax.axis_size("head")
    my_head = lax.axis_index("head")
    q_width = queries.shape[1] // head_devices
    kv_width = keys.shape[1] // head_devices

    def columns_for(dest):
        q_part = lax.dynamic_slice_in_dim(queries, dest * q_width, q_width, 1)
        k_part = lax.dynamic_slice_in_dim(keys, dest * kv_width, kv_width, 1)
        v_part = lax.dynamic_slice_in_dim(values, dest * kv_width, kv_width, 1)
        return jnp.concatenate([q_part, k_part, v_part], 1)

    received = [columns_for(my_head)]
    for k in range(1, head_devices):
        received.append(shifted(columns_for((my_head + k) % head_devices), "head", k))
    total = scatter_sum(both, seq_devices)
    total, received = lax.optimization_barrier((total, received))
    by_shift = jnp.stack(received, 0)
    order = (my_head - jnp.arange(head_devices, dtype=jnp.int32)) % head_devices
    tokens = by_shift[order].reshape(-1, q_width + 2 * kv_width)
    q_local = tokens[:, :q_width]
    kv_local = jnp.stack([tokens[:, q_width:q_width + kv_width], tokens[:, q_width + kv_width:]], 0)
    tail_cache = jnp.stack([prefix_keys[cache_rows - WIN:], prefix_values[cache_rows - WIN:]], 0)
    outgoing = jnp.where(my_seq == seq_devices - 1, tail_cache, kv_local)
    prev_kv = shifted(outgoing, "seq", 1)
    side = gather_sums(total, both.shape, seq_devices)

    slot_l = jnp.where(is_ret, slot, 0).astype(jnp.int32)
    return attend(
        roles.astype(jnp.int32),
        slot_l,
        col_count.astype(jnp.int32),
        diagonals.reshape(heads * NSL).astype(jnp.int32),
        q_local,
        prev_kv,
        kv_local,
        side,
    )


def solution(mesh):
    placed = (
        P(("seq", "head"), None),
        P(("seq", "head"), None),
        P(("seq", "head"), None),
        P("seq", "head"),
        P("seq", "head"),
        P("head"),
        P("head", None),
        P("head"),
        P("head", None),
    )
    return jax.shard_map(
        shards, mesh=mesh, in_specs=placed, out_specs=P("seq", "head"), check_vma=False
    )
```

```python
import functools
import math

import jax
import jax.numpy as jnp
from jax import lax
from jax.experimental import pallas as pl
from jax.experimental.pallas import tpu as pltpu
from jax.sharding import PartitionSpec as P

QUERY_HEADS = 64
KEY_VALUE_HEADS = 8
HEAD_SIZE = 128
SINK = 128
WIN = 512
BLK = 64
VB = 6
NSL = 4
MAX_RETRIEVERS = 4


def shifted(block, axis, distance):
    devices = range(lax.axis_size(axis))
    route = [((i - distance) % len(devices), i) for i in devices]
    return lax.ppermute(block, axis, route)


def exact_dot(weights, vals):
    hi = weights.astype(jnp.bfloat16)
    lo = (weights - hi.astype(jnp.float32)).astype(jnp.bfloat16)
    out = jnp.dot(hi, vals, preferred_element_type=jnp.float32)
    return out + jnp.dot(lo, vals, preferred_element_type=jnp.float32)


def local_kernel(roles_ref, diag_ref, q_ref, prev_ref, own_ref, o_ref, m_ref, l_ref):
    h = pl.program_id(0)
    rows = q_ref.shape[0]
    scaling = 1.0 / math.sqrt(HEAD_SIZE)
    q = q_ref[...]
    dims = (((1,), (1,)), ((), ()))

    def scores(keys):
        return lax.dot_general(q, keys, dims, preferred_element_type=jnp.float32) * scaling

    s_prev = scores(prev_ref[0])
    s_own = scores(own_ref[0])
    row = lax.broadcasted_iota(jnp.int32, (rows, rows), 0)
    col = lax.broadcasted_iota(jnp.int32, (rows, rows), 1)

    def finish(ok_prev, ok_own):
        neg = -jnp.inf
        m = jnp.maximum(jnp.max(jnp.where(ok_prev, s_prev, neg), axis=1, keepdims=True),
                        jnp.max(jnp.where(ok_own, s_own, neg), axis=1, keepdims=True))
        e_prev = jnp.where(ok_prev, jnp.exp(s_prev - m), 0.0)
        e_own = jnp.where(ok_own, jnp.exp(s_own - m), 0.0)
        total = jnp.sum(e_prev, axis=1, keepdims=True) + jnp.sum(e_own, axis=1, keepdims=True)
        o_ref[...] = exact_dot(e_prev, prev_ref[1]) + exact_dot(e_own, own_ref[1])
        m_ref[...] = jnp.broadcast_to(m, m_ref.shape)
        l_ref[...] = jnp.broadcast_to(total, l_ref.shape)

    @pl.when(roles_ref[h] != 1)
    def _():
        finish(col > row, col <= row)

    @pl.when(roles_ref[h] == 1)
    def _():
        rel_prev = row // BLK + rows // BLK - col // BLK
        rel_own = row // BLK - col // BLK
        ok_prev = jnp.zeros((rows, rows), jnp.bool_)
        ok_own = jnp.zeros((rows, rows), jnp.bool_)
        for d in range(NSL):
            off = diag_ref[h * NSL + d]
            ok_prev = ok_prev | (rel_prev == off)
            ok_own = ok_own | ((rel_own == off) & ((off > 0) | (col <= row)))
        finish(ok_prev, ok_own)


def side_kernel(roles_ref, slot_ref, count_ref, q_ref, o_loc_ref, m_ref, l_ref,
                vk_ref, vv_ref, sk_ref, sv_ref, o_ref):
    h = pl.program_id(0)
    scaling = 1.0 / math.sqrt(HEAD_SIZE)
    q = q_ref[...]
    dims = (((1,), (1,)), ((), ()))

    def merge(keys, vals, ok):
        s = lax.dot_general(q, keys, dims, preferred_element_type=jnp.float32) * scaling
        m_loc = m_ref[:, 0:1]
        m = jnp.maximum(m_loc, jnp.max(jnp.where(ok, s, -jnp.inf), axis=1, keepdims=True))
        e = jnp.where(ok, jnp.exp(s - m), 0.0)
        scale_loc = jnp.exp(m_loc - m)
        total = l_ref[:, 0:1] * scale_loc + jnp.sum(e, axis=1, keepdims=True)
        out = o_loc_ref[...] * scale_loc + exact_dot(e, vals)
        o_ref[...] = (out / total).astype(o_ref.dtype)

    @pl.when(roles_ref[h] != 1)
    def _():
        merge(sk_ref[...], sv_ref[...], jnp.ones((q.shape[0], sk_ref.shape[0]), jnp.bool_))

    @pl.when(roles_ref[h] == 1)
    def _():
        side_col = lax.broadcasted_iota(jnp.int32, (q.shape[0], vk_ref.shape[0]), 1)
        merge(vk_ref[...], vv_ref[...], side_col // BLK < count_ref[h])


def attend_local(roles_l, diag_l, q_local, prev_kv, own_kv):
    rows = q_local.shape[0]
    heads = q_local.shape[1] // HEAD_SIZE
    grid_spec = pltpu.PrefetchScalarGridSpec(
        num_scalar_prefetch=2,
        grid=(heads,),
        in_specs=[
            pl.BlockSpec((rows, HEAD_SIZE), lambda h, *_: (0, h)),
            pl.BlockSpec((2, rows, HEAD_SIZE), lambda h, *_: (0, 0, 0)),
            pl.BlockSpec((2, rows, HEAD_SIZE), lambda h, *_: (0, 0, 0)),
        ],
        out_specs=[
            pl.BlockSpec((rows, HEAD_SIZE), lambda h, *_: (0, h)),
            pl.BlockSpec((None, rows, HEAD_SIZE), lambda h, *_: (h, 0, 0)),
            pl.BlockSpec((None, rows, HEAD_SIZE), lambda h, *_: (h, 0, 0)),
        ],
    )
    return pl.pallas_call(
        local_kernel,
        grid_spec=grid_spec,
        out_shape=[
            jax.ShapeDtypeStruct(q_local.shape, jnp.float32),
            jax.ShapeDtypeStruct((heads, rows, HEAD_SIZE), jnp.float32),
            jax.ShapeDtypeStruct((heads, rows, HEAD_SIZE), jnp.float32),
        ],
    )(roles_l, diag_l, q_local, prev_kv, own_kv)


def attend_side(roles_l, slot_l, count_l, q_local, o_loc, m_loc, l_loc, side):
    rows = q_local.shape[0]
    heads = q_local.shape[1] // HEAD_SIZE
    vrows = VB * BLK
    sink_block = MAX_RETRIEVERS * vrows // SINK
    grid_spec = pltpu.PrefetchScalarGridSpec(
        num_scalar_prefetch=3,
        grid=(heads,),
        in_specs=[
            pl.BlockSpec((rows, HEAD_SIZE), lambda h, *_: (0, h)),
            pl.BlockSpec((rows, HEAD_SIZE), lambda h, *_: (0, h)),
            pl.BlockSpec((None, rows, HEAD_SIZE), lambda h, *_: (h, 0, 0)),
            pl.BlockSpec((None, rows, HEAD_SIZE), lambda h, *_: (h, 0, 0)),
            pl.BlockSpec((None, vrows, HEAD_SIZE), lambda h, r, s, *_: (0, s[h], 0)),
            pl.BlockSpec((None, vrows, HEAD_SIZE), lambda h, r, s, *_: (1, s[h], 0)),
            pl.BlockSpec((None, SINK, HEAD_SIZE), lambda h, *_: (0, sink_block, 0)),
            pl.BlockSpec((None, SINK, HEAD_SIZE), lambda h, *_: (1, sink_block, 0)),
        ],
        out_specs=pl.BlockSpec((rows, HEAD_SIZE), lambda h, *_: (0, h)),
    )
    return pl.pallas_call(
        side_kernel,
        grid_spec=grid_spec,
        out_shape=jax.ShapeDtypeStruct(q_local.shape, jnp.bfloat16),
    )(roles_l, slot_l, count_l, q_local, o_loc, m_loc, l_loc, side, side, side, side)


def scatter_sum(block, seq_devices):
    flat = block.reshape(seq_devices, -1, block.shape[-1])
    mine = lax.all_to_all(flat, "seq", 0, 0, tiled=True)
    return jnp.sum(mine.astype(jnp.float32), 0, keepdims=True).astype(block.dtype)


def gather_sums(total, shape, seq_devices):
    every = lax.all_to_all(jnp.broadcast_to(total, (seq_devices,) + total.shape[1:]), "seq", 0, 0, tiled=True)
    return every.reshape(shape)


def shards(queries, keys, values, prefix_keys, prefix_values, roles, columns, col_count, diagonals):
    seq_devices = lax.axis_size("seq")
    my_seq = lax.axis_index("seq")
    cache_rows = prefix_keys.shape[0]
    blocks_dev = cache_rows // BLK
    heads = roles.shape[0]

    is_ret = roles == 1
    slot = jnp.cumsum(is_ret.astype(jnp.int32)) - 1
    match = is_ret[None, :] & (slot[None, :] == jnp.arange(MAX_RETRIEVERS, dtype=jnp.int32)[:, None])
    head_of_slot = jnp.argmax(match, axis=1)
    cols_s = columns[head_of_slot]
    owner = cols_s // blocks_dev
    local_block = cols_s - owner * blocks_dev
    mine = (owner == my_seq)[:, :, None, None]
    kv_blocks = jnp.stack([prefix_keys, prefix_values], 0).reshape(2, blocks_dev, BLK, HEAD_SIZE)
    pieces = kv_blocks[:, local_block]
    pieces = jnp.where(mine[None], pieces, jnp.zeros_like(pieces))
    pieces = pieces.reshape(2, MAX_RETRIEVERS * VB * BLK, HEAD_SIZE)
    sink = jnp.stack([prefix_keys[:SINK], prefix_values[:SINK]], 0)
    sink = jnp.where(my_seq == 0, sink, jnp.zeros_like(sink))
    both = jnp.concatenate([pieces, sink], 1)

    head_devices = lax.axis_size("head")
    my_head = lax.axis_index("head")
    q_width = queries.shape[1] // head_devices
    kv_width = keys.shape[1] // head_devices

    def columns_for(dest):
        q_part = lax.dynamic_slice_in_dim(queries, dest * q_width, q_width, 1)
        k_part = lax.dynamic_slice_in_dim(keys, dest * kv_width, kv_width, 1)
        v_part = lax.dynamic_slice_in_dim(values, dest * kv_width, kv_width, 1)
        return jnp.concatenate([q_part, k_part, v_part], 1)

    received = [columns_for(my_head)]
    for k in range(1, head_devices):
        received.append(shifted(columns_for((my_head + k) % head_devices), "head", k))
    total = scatter_sum(both, seq_devices)
    total, received = lax.optimization_barrier((total, received))
    by_shift = jnp.stack(received, 0)
    order = (my_head - jnp.arange(head_devices, dtype=jnp.int32)) % head_devices
    tokens = by_shift[order].reshape(-1, q_width + 2 * kv_width)
    q_local = tokens[:, :q_width]
    kv_local = jnp.stack([tokens[:, q_width:q_width + kv_width], tokens[:, q_width + kv_width:]], 0)
    tail_cache = jnp.stack([prefix_keys[cache_rows - WIN:], prefix_values[cache_rows - WIN:]], 0)
    outgoing = jnp.where(my_seq == seq_devices - 1, tail_cache, kv_local)
    prev_kv = shifted(outgoing, "seq", 1)
    side = gather_sums(total, both.shape, seq_devices)

    slot_l = jnp.where(is_ret, slot, 0).astype(jnp.int32)
    roles_l = roles.astype(jnp.int32)
    o_loc, m_loc, l_loc = attend_local(
        roles_l, diagonals.reshape(heads * NSL).astype(jnp.int32), q_local, prev_kv, kv_local)
    return attend_side(roles_l, slot_l, col_count.astype(jnp.int32), q_local, o_loc, m_loc, l_loc, side)


def solution(mesh):
    placed = (
        P(("seq", "head"), None),
        P(("seq", "head"), None),
        P(("seq", "head"), None),
        P("seq", "head"),
        P("seq", "head"),
        P("head"),
        P("head", None),
        P("head"),
        P("head", None),
    )
    return jax.shard_map(
        shards, mesh=mesh, in_specs=placed, out_specs=P("seq", "head"), check_vma=False
    )
```

```python
import functools
import math

import jax
import jax.numpy as jnp
from jax import lax
from jax.experimental import pallas as pl
from jax.experimental.pallas import tpu as pltpu
from jax.sharding import PartitionSpec as P

QUERY_HEADS = 64
KEY_VALUE_HEADS = 8
HEAD_SIZE = 128
SINK = 128
WIN = 512
BLK = 64
VB = 6
NSL = 4
MAX_RETRIEVERS = 4


def shifted(block, axis, distance):
    devices = range(lax.axis_size(axis))
    route = [((i - distance) % len(devices), i) for i in devices]
    return lax.ppermute(block, axis, route)


def exact_dot(weights, vals):
    hi = weights.astype(jnp.bfloat16)
    lo = (weights - hi.astype(jnp.float32)).astype(jnp.bfloat16)
    out = jnp.dot(hi, vals, preferred_element_type=jnp.float32)
    return out + jnp.dot(lo, vals, preferred_element_type=jnp.float32)


def local_kernel(roles_ref, diag_ref, q_ref, prev_ref, own_ref, o_ref, m_ref, l_ref):
    h = pl.program_id(0)
    rows = q_ref.shape[0]
    scaling = 1.0 / math.sqrt(HEAD_SIZE)
    q = q_ref[...]
    dims = (((1,), (1,)), ((), ()))

    def scores(keys):
        return lax.dot_general(q, keys, dims, preferred_element_type=jnp.float32) * scaling

    s_prev = scores(prev_ref[0])
    s_own = scores(own_ref[0])
    row = lax.broadcasted_iota(jnp.int32, (rows, rows), 0)
    col = lax.broadcasted_iota(jnp.int32, (rows, rows), 1)

    def finish(ok_prev, ok_own):
        neg = -jnp.inf
        m = jnp.maximum(jnp.max(jnp.where(ok_prev, s_prev, neg), axis=1, keepdims=True),
                        jnp.max(jnp.where(ok_own, s_own, neg), axis=1, keepdims=True))
        e_prev = jnp.where(ok_prev, jnp.exp(s_prev - m), 0.0)
        e_own = jnp.where(ok_own, jnp.exp(s_own - m), 0.0)
        total = jnp.sum(e_prev, axis=1, keepdims=True) + jnp.sum(e_own, axis=1, keepdims=True)
        o_ref[...] = exact_dot(e_prev, prev_ref[1]) + exact_dot(e_own, own_ref[1])
        m_ref[...] = jnp.broadcast_to(m, m_ref.shape)
        l_ref[...] = jnp.broadcast_to(total, l_ref.shape)

    @pl.when(roles_ref[h] != 1)
    def _():
        finish(col > row, col <= row)

    @pl.when(roles_ref[h] == 1)
    def _():
        rel_prev = row // BLK + rows // BLK - col // BLK
        rel_own = row // BLK - col // BLK
        ok_prev = jnp.zeros((rows, rows), jnp.bool_)
        ok_own = jnp.zeros((rows, rows), jnp.bool_)
        for d in range(NSL):
            off = diag_ref[h * NSL + d]
            ok_prev = ok_prev | (rel_prev == off)
            ok_own = ok_own | ((rel_own == off) & ((off > 0) | (col <= row)))
        finish(ok_prev, ok_own)


def side_kernel(roles_ref, slot_ref, count_ref, q_ref, o_loc_ref, m_ref, l_ref,
                vk_ref, vv_ref, sk_ref, sv_ref, o_ref):
    h = pl.program_id(0)
    scaling = 1.0 / math.sqrt(HEAD_SIZE)
    q = q_ref[...]
    dims = (((1,), (1,)), ((), ()))

    def merge(keys, vals, ok):
        s = lax.dot_general(q, keys, dims, preferred_element_type=jnp.float32) * scaling
        m_loc = m_ref[:, 0:1]
        m = jnp.maximum(m_loc, jnp.max(jnp.where(ok, s, -jnp.inf), axis=1, keepdims=True))
        e = jnp.where(ok, jnp.exp(s - m), 0.0)
        scale_loc = jnp.exp(m_loc - m)
        total = l_ref[:, 0:1] * scale_loc + jnp.sum(e, axis=1, keepdims=True)
        out = o_loc_ref[...] * scale_loc + exact_dot(e, vals)
        o_ref[...] = (out / total).astype(o_ref.dtype)

    @pl.when(roles_ref[h] != 1)
    def _():
        merge(sk_ref[...], sv_ref[...], jnp.ones((q.shape[0], sk_ref.shape[0]), jnp.bool_))

    @pl.when(roles_ref[h] == 1)
    def _():
        side_col = lax.broadcasted_iota(jnp.int32, (q.shape[0], vk_ref.shape[0]), 1)
        merge(vk_ref[...], vv_ref[...], side_col // BLK < count_ref[h])


def attend_local(roles_l, diag_l, q_local, prev_kv, own_kv):
    rows = q_local.shape[0]
    heads = q_local.shape[1] // HEAD_SIZE
    grid_spec = pltpu.PrefetchScalarGridSpec(
        num_scalar_prefetch=2,
        grid=(heads,),
        in_specs=[
            pl.BlockSpec((rows, HEAD_SIZE), lambda h, *_: (0, h)),
            pl.BlockSpec((2, rows, HEAD_SIZE), lambda h, *_: (0, 0, 0)),
            pl.BlockSpec((2, rows, HEAD_SIZE), lambda h, *_: (0, 0, 0)),
        ],
        out_specs=[
            pl.BlockSpec((rows, HEAD_SIZE), lambda h, *_: (0, h)),
            pl.BlockSpec((None, rows, HEAD_SIZE), lambda h, *_: (h, 0, 0)),
            pl.BlockSpec((None, rows, HEAD_SIZE), lambda h, *_: (h, 0, 0)),
        ],
    )
    return pl.pallas_call(
        local_kernel,
        grid_spec=grid_spec,
        out_shape=[
            jax.ShapeDtypeStruct(q_local.shape, jnp.float32),
            jax.ShapeDtypeStruct((heads, rows, HEAD_SIZE), jnp.float32),
            jax.ShapeDtypeStruct((heads, rows, HEAD_SIZE), jnp.float32),
        ],
    )(roles_l, diag_l, q_local, prev_kv, own_kv)


def attend_side(roles_l, slot_l, count_l, q_local, o_loc, m_loc, l_loc, side):
    rows = q_local.shape[0]
    heads = q_local.shape[1] // HEAD_SIZE
    vrows = VB * BLK
    sink_block = MAX_RETRIEVERS * vrows // SINK
    grid_spec = pltpu.PrefetchScalarGridSpec(
        num_scalar_prefetch=3,
        grid=(heads,),
        in_specs=[
            pl.BlockSpec((rows, HEAD_SIZE), lambda h, *_: (0, h)),
            pl.BlockSpec((rows, HEAD_SIZE), lambda h, *_: (0, h)),
            pl.BlockSpec((None, rows, HEAD_SIZE), lambda h, *_: (h, 0, 0)),
            pl.BlockSpec((None, rows, HEAD_SIZE), lambda h, *_: (h, 0, 0)),
            pl.BlockSpec((None, vrows, HEAD_SIZE), lambda h, r, s, *_: (0, s[h], 0)),
            pl.BlockSpec((None, vrows, HEAD_SIZE), lambda h, r, s, *_: (1, s[h], 0)),
            pl.BlockSpec((None, SINK, HEAD_SIZE), lambda h, *_: (0, sink_block, 0)),
            pl.BlockSpec((None, SINK, HEAD_SIZE), lambda h, *_: (1, sink_block, 0)),
        ],
        out_specs=pl.BlockSpec((rows, HEAD_SIZE), lambda h, *_: (0, h)),
    )
    return pl.pallas_call(
        side_kernel,
        grid_spec=grid_spec,
        out_shape=jax.ShapeDtypeStruct(q_local.shape, jnp.bfloat16),
    )(roles_l, slot_l, count_l, q_local, o_loc, m_loc, l_loc, side, side, side, side)


def scatter_sum(block, seq_devices):
    flat = block.reshape(seq_devices, -1, block.shape[-1])
    mine = lax.all_to_all(flat, "seq", 0, 0, tiled=True)
    return jnp.sum(mine.astype(jnp.float32), 0, keepdims=True).astype(block.dtype)


def gather_sums(total, shape, seq_devices):
    every = lax.all_to_all(jnp.broadcast_to(total, (seq_devices,) + total.shape[1:]), "seq", 0, 0, tiled=True)
    return every.reshape(shape)


def shards(queries, keys, values, prefix_keys, prefix_values, roles, columns, col_count, diagonals):
    seq_devices = lax.axis_size("seq")
    my_seq = lax.axis_index("seq")
    cache_rows = prefix_keys.shape[0]
    blocks_dev = cache_rows // BLK
    heads = roles.shape[0]

    is_ret = roles == 1
    slot = jnp.cumsum(is_ret.astype(jnp.int32)) - 1
    match = is_ret[None, :] & (slot[None, :] == jnp.arange(MAX_RETRIEVERS, dtype=jnp.int32)[:, None])
    head_of_slot = jnp.argmax(match, axis=1)
    cols_s = columns[head_of_slot]
    owner = cols_s // blocks_dev
    local_block = cols_s - owner * blocks_dev
    mine = (owner == my_seq)[:, :, None, None]
    kv_blocks = jnp.stack([prefix_keys, prefix_values], 0).reshape(2, blocks_dev, BLK, HEAD_SIZE)
    pieces = kv_blocks[:, local_block]
    pieces = jnp.where(mine[None], pieces, jnp.zeros_like(pieces))
    pieces = pieces.reshape(2, MAX_RETRIEVERS * VB * BLK, HEAD_SIZE)
    sink = jnp.stack([prefix_keys[:SINK], prefix_values[:SINK]], 0)
    sink = jnp.where(my_seq == 0, sink, jnp.zeros_like(sink))
    both = jnp.concatenate([pieces, sink], 1)

    head_devices = lax.axis_size("head")
    my_head = lax.axis_index("head")
    q_width = queries.shape[1] // head_devices
    kv_width = keys.shape[1] // head_devices

    def columns_for(dest):
        q_part = lax.dynamic_slice_in_dim(queries, dest * q_width, q_width, 1)
        k_part = lax.dynamic_slice_in_dim(keys, dest * kv_width, kv_width, 1)
        v_part = lax.dynamic_slice_in_dim(values, dest * kv_width, kv_width, 1)
        return jnp.concatenate([q_part, k_part, v_part], 1)

    received = [columns_for(my_head)]
    for k in range(1, head_devices):
        received.append(shifted(columns_for((my_head + k) % head_devices), "head", k))
    earlier = []
    for k in range(head_devices):
        route = [(sp * head_devices + j, (sp + 1) * head_devices + (j + k) % head_devices)
                 for sp in range(seq_devices - 1) for j in range(head_devices)]
        part = columns_for((my_head + k) % head_devices)[:, q_width:]
        earlier.append(lax.ppermute(part, ("seq", "head"), route))
    tail_cache = jnp.concatenate([prefix_keys[cache_rows - WIN:], prefix_values[cache_rows - WIN:]], 1)
    cache_tail = lax.ppermute(tail_cache, "seq", [(seq_devices - 1, 0)])
    total = scatter_sum(both, seq_devices)
    total, received, earlier, cache_tail = lax.optimization_barrier((total, received, earlier, cache_tail))
    order = (my_head - jnp.arange(head_devices, dtype=jnp.int32)) % head_devices
    tokens = jnp.stack(received, 0)[order].reshape(-1, q_width + 2 * kv_width)
    q_local = tokens[:, :q_width]
    kv_local = jnp.stack([tokens[:, q_width:q_width + kv_width], tokens[:, q_width + kv_width:]], 0)
    before = jnp.stack(earlier, 0)[order].reshape(-1, 2 * kv_width)
    before = jnp.where(my_seq == 0, cache_tail, before)
    prev_kv = jnp.stack([before[:, :kv_width], before[:, kv_width:]], 0)
    side = gather_sums(total, both.shape, seq_devices)

    slot_l = jnp.where(is_ret, slot, 0).astype(jnp.int32)
    roles_l = roles.astype(jnp.int32)
    o_loc, m_loc, l_loc = attend_local(
        roles_l, diagonals.reshape(heads * NSL).astype(jnp.int32), q_local, prev_kv, kv_local)
    return attend_side(roles_l, slot_l, col_count.astype(jnp.int32), q_local, o_loc, m_loc, l_loc, side)


def solution(mesh):
    placed = (
        P(("seq", "head"), None),
        P(("seq", "head"), None),
        P(("seq", "head"), None),
        P("seq", "head"),
        P("seq", "head"),
        P("head"),
        P("head", None),
        P("head"),
        P("head", None),
    )
    return jax.shard_map(
        shards, mesh=mesh, in_specs=placed, out_specs=P("seq", "head"), check_vma=False
    )
```

```python
import functools
import math

import jax
import jax.numpy as jnp
from jax import lax
from jax.experimental import pallas as pl
from jax.experimental.pallas import tpu as pltpu
from jax.sharding import PartitionSpec as P

QUERY_HEADS = 64
KEY_VALUE_HEADS = 8
HEAD_SIZE = 128
SINK = 128
WIN = 512
BLK = 64
VB = 6
NSL = 4
MAX_RETRIEVERS = 4


def shifted(block, axis, distance):
    devices = range(lax.axis_size(axis))
    route = [((i - distance) % len(devices), i) for i in devices]
    return lax.ppermute(block, axis, route)


def attend_kernel(roles_ref, slot_ref, count_ref, diag_ref,
                  q_ref, prev_ref, own_ref, vk_ref, vv_ref, sk_ref, sv_ref, o_ref):
    h = pl.program_id(0)
    rows = q_ref.shape[0]
    half = rows // 2
    scaling = 1.0 / math.sqrt(HEAD_SIZE)
    dims = (((1,), (1,)), ((), ()))
    neg = -jnp.inf

    def scores(q, keys):
        return lax.dot_general(q, keys, dims, preferred_element_type=jnp.float32) * scaling

    def one_half(part, role_ret):
        r0 = part * half
        p0 = part * half
        p1 = rows
        w_own = half + part * half
        q = q_ref[r0:r0 + half, :]
        s_prev = scores(q, prev_ref[0, p0:p1, :])
        s_own = scores(q, own_ref[0, 0:w_own, :])
        row_p = lax.broadcasted_iota(jnp.int32, s_prev.shape, 0) + r0
        col_p = lax.broadcasted_iota(jnp.int32, s_prev.shape, 1) + p0
        row_o = lax.broadcasted_iota(jnp.int32, s_own.shape, 0) + r0
        col_o = lax.broadcasted_iota(jnp.int32, s_own.shape, 1)
        if role_ret:
            s_side = scores(q, vk_ref[...])
            v_side = vv_ref[...]
            side_col = lax.broadcasted_iota(jnp.int32, s_side.shape, 1)
            ok_side = side_col // BLK < count_ref[h]
            rel_prev = row_p // BLK + rows // BLK - col_p // BLK
            rel_own = row_o // BLK - col_o // BLK
            ok_prev = jnp.zeros(s_prev.shape, jnp.bool_)
            ok_own = jnp.zeros(s_own.shape, jnp.bool_)
            for d in range(NSL):
                off = diag_ref[h * NSL + d]
                ok_prev = ok_prev | (rel_prev == off)
                ok_own = ok_own | ((rel_own == off) & ((off > 0) | (col_o <= row_o)))
        else:
            s_side = scores(q, sk_ref[...])
            v_side = sv_ref[...]
            ok_side = jnp.ones(s_side.shape, jnp.bool_)
            ok_prev = col_p > row_p
            ok_own = col_o <= row_o
        m_side = jnp.max(jnp.where(ok_side, s_side, neg), axis=1, keepdims=True)
        m_prev = jnp.max(jnp.where(ok_prev, s_prev, neg), axis=1, keepdims=True)
        m_own = jnp.max(jnp.where(ok_own, s_own, neg), axis=1, keepdims=True)
        m = jnp.maximum(jnp.maximum(m_side, m_prev), m_own)
        e_side = jnp.where(ok_side, jnp.exp(s_side - m), 0.0)
        e_prev = jnp.where(ok_prev, jnp.exp(s_prev - m), 0.0)
        e_own = jnp.where(ok_own, jnp.exp(s_own - m), 0.0)
        total = (jnp.sum(e_side, axis=1, keepdims=True)
                 + jnp.sum(e_prev, axis=1, keepdims=True)
                 + jnp.sum(e_own, axis=1, keepdims=True))
        p_side = (e_side / total).astype(jnp.bfloat16)
        p_prev = (e_prev / total).astype(jnp.bfloat16)
        p_own = (e_own / total).astype(jnp.bfloat16)
        out = jnp.dot(p_side, v_side, preferred_element_type=jnp.float32)
        out = out + jnp.dot(p_prev, prev_ref[1, p0:p1, :], preferred_element_type=jnp.float32)
        out = out + jnp.dot(p_own, own_ref[1, 0:w_own, :], preferred_element_type=jnp.float32)
        o_ref[r0:r0 + half, :] = out.astype(o_ref.dtype)

    @pl.when(roles_ref[h] != 1)
    def _():
        one_half(0, False)
        one_half(1, False)

    @pl.when(roles_ref[h] == 1)
    def _():
        one_half(0, True)
        one_half(1, True)


def attend(roles_l, slot_l, count_l, diag_l, q_local, prev_kv, own_kv, side):
    rows = q_local.shape[0]
    heads = q_local.shape[1] // HEAD_SIZE
    vrows = VB * BLK
    sink_block = MAX_RETRIEVERS * vrows // SINK
    grid_spec = pltpu.PrefetchScalarGridSpec(
        num_scalar_prefetch=4,
        grid=(heads,),
        in_specs=[
            pl.BlockSpec((rows, HEAD_SIZE), lambda h, *_: (0, h)),
            pl.BlockSpec((2, rows, HEAD_SIZE), lambda h, *_: (0, 0, 0)),
            pl.BlockSpec((2, rows, HEAD_SIZE), lambda h, *_: (0, 0, 0)),
            pl.BlockSpec((None, vrows, HEAD_SIZE), lambda h, r, s, *_: (0, s[h], 0)),
            pl.BlockSpec((None, vrows, HEAD_SIZE), lambda h, r, s, *_: (1, s[h], 0)),
            pl.BlockSpec((None, SINK, HEAD_SIZE), lambda h, *_: (0, sink_block, 0)),
            pl.BlockSpec((None, SINK, HEAD_SIZE), lambda h, *_: (1, sink_block, 0)),
        ],
        out_specs=pl.BlockSpec((rows, HEAD_SIZE), lambda h, *_: (0, h)),
    )
    return pl.pallas_call(
        attend_kernel,
        grid_spec=grid_spec,
        out_shape=jax.ShapeDtypeStruct(q_local.shape, jnp.bfloat16),
    )(roles_l, slot_l, count_l, diag_l, q_local, prev_kv, own_kv, side, side, side, side)


def scatter_sum(block, seq_devices):
    flat = block.reshape(seq_devices, -1, block.shape[-1])
    mine = lax.all_to_all(flat, "seq", 0, 0, tiled=True)
    return jnp.sum(mine.astype(jnp.float32), 0, keepdims=True).astype(block.dtype)


def gather_sums(total, shape, seq_devices):
    every = lax.all_to_all(jnp.broadcast_to(total, (seq_devices,) + total.shape[1:]), "seq", 0, 0, tiled=True)
    return every.reshape(shape)


def shards(queries, keys, values, prefix_keys, prefix_values, roles, columns, col_count, diagonals):
    seq_devices = lax.axis_size("seq")
    my_seq = lax.axis_index("seq")
    cache_rows = prefix_keys.shape[0]
    blocks_dev = cache_rows // BLK
    heads = roles.shape[0]

    is_ret = roles == 1
    slot = jnp.cumsum(is_ret.astype(jnp.int32)) - 1
    match = is_ret[None, :] & (slot[None, :] == jnp.arange(MAX_RETRIEVERS, dtype=jnp.int32)[:, None])
    head_of_slot = jnp.argmax(match, axis=1)
    cols_s = columns[head_of_slot]
    owner = cols_s // blocks_dev
    local_block = cols_s - owner * blocks_dev
    mine = (owner == my_seq)[:, :, None, None]
    kv_blocks = jnp.stack([prefix_keys, prefix_values], 0).reshape(2, blocks_dev, BLK, HEAD_SIZE)
    pieces = kv_blocks[:, local_block]
    pieces = jnp.where(mine[None], pieces, jnp.zeros_like(pieces))
    pieces = pieces.reshape(2, MAX_RETRIEVERS * VB * BLK, HEAD_SIZE)
    sink = jnp.stack([prefix_keys[:SINK], prefix_values[:SINK]], 0)
    sink = jnp.where(my_seq == 0, sink, jnp.zeros_like(sink))
    both = jnp.concatenate([pieces, sink], 1)

    head_devices = lax.axis_size("head")
    my_head = lax.axis_index("head")
    q_width = queries.shape[1] // head_devices
    kv_width = keys.shape[1] // head_devices

    def columns_for(dest):
        q_part = lax.dynamic_slice_in_dim(queries, dest * q_width, q_width, 1)
        k_part = lax.dynamic_slice_in_dim(keys, dest * kv_width, kv_width, 1)
        v_part = lax.dynamic_slice_in_dim(values, dest * kv_width, kv_width, 1)
        return jnp.concatenate([q_part, k_part, v_part], 1)

    received = [columns_for(my_head)]
    for k in range(1, head_devices):
        received.append(shifted(columns_for((my_head + k) % head_devices), "head", k))
    total = scatter_sum(both, seq_devices)
    total, received = lax.optimization_barrier((total, received))
    by_shift = jnp.stack(received, 0)
    order = (my_head - jnp.arange(head_devices, dtype=jnp.int32)) % head_devices
    tokens = by_shift[order].reshape(-1, q_width + 2 * kv_width)
    q_local = tokens[:, :q_width]
    kv_local = jnp.stack([tokens[:, q_width:q_width + kv_width], tokens[:, q_width + kv_width:]], 0)
    tail_cache = jnp.stack([prefix_keys[cache_rows - WIN:], prefix_values[cache_rows - WIN:]], 0)
    outgoing = jnp.where(my_seq == seq_devices - 1, tail_cache, kv_local)
    prev_kv = shifted(outgoing, "seq", 1)
    side = gather_sums(total, both.shape, seq_devices)

    slot_l = jnp.where(is_ret, slot, 0).astype(jnp.int32)
    return attend(
        roles.astype(jnp.int32),
        slot_l,
        col_count.astype(jnp.int32),
        diagonals.reshape(heads * NSL).astype(jnp.int32),
        q_local,
        prev_kv,
        kv_local,
        side,
    )


def solution(mesh):
    placed = (
        P(("seq", "head"), None),
        P(("seq", "head"), None),
        P(("seq", "head"), None),
        P("seq", "head"),
        P("seq", "head"),
        P("head"),
        P("head", None),
        P("head"),
        P("head", None),
    )
    return jax.shard_map(
        shards, mesh=mesh, in_specs=placed, out_specs=P("seq", "head"), check_vma=False
    )
```

```python
import functools
import math

import jax
import jax.numpy as jnp
from jax import lax
from jax.experimental import pallas as pl
from jax.experimental.pallas import tpu as pltpu
from jax.sharding import PartitionSpec as P

QUERY_HEADS = 64
KEY_VALUE_HEADS = 8
HEAD_SIZE = 128
SINK = 128
WIN = 512
BLK = 64
VB = 6
NSL = 4
MAX_RETRIEVERS = 4


def shifted(block, axis, distance):
    devices = range(lax.axis_size(axis))
    route = [((i - distance) % len(devices), i) for i in devices]
    return lax.ppermute(block, axis, route)


def attend_kernel(roles_ref, slot_ref, count_ref, diag_ref,
                  q_ref, prev_ref, own_ref, vk_ref, vv_ref, sk_ref, sv_ref, o_ref):
    h = pl.program_id(0)
    rows = q_ref.shape[0]
    parts = 4
    half = rows // parts
    scaling = 1.0 / math.sqrt(HEAD_SIZE)
    dims = (((1,), (1,)), ((), ()))
    neg = -jnp.inf

    def scores(q, keys):
        return lax.dot_general(q, keys, dims, preferred_element_type=jnp.float32) * scaling

    def one_half(part, role_ret):
        r0 = part * half
        p0 = part * half
        p1 = rows
        w_own = (part + 1) * half
        q = q_ref[r0:r0 + half, :]
        s_prev = scores(q, prev_ref[0, p0:p1, :])
        s_own = scores(q, own_ref[0, 0:w_own, :])
        row_p = lax.broadcasted_iota(jnp.int32, s_prev.shape, 0) + r0
        col_p = lax.broadcasted_iota(jnp.int32, s_prev.shape, 1) + p0
        row_o = lax.broadcasted_iota(jnp.int32, s_own.shape, 0) + r0
        col_o = lax.broadcasted_iota(jnp.int32, s_own.shape, 1)
        if role_ret:
            s_side = scores(q, vk_ref[...])
            v_side = vv_ref[...]
            side_col = lax.broadcasted_iota(jnp.int32, s_side.shape, 1)
            ok_side = side_col // BLK < count_ref[h]
            rel_prev = row_p // BLK + rows // BLK - col_p // BLK
            rel_own = row_o // BLK - col_o // BLK
            ok_prev = jnp.zeros(s_prev.shape, jnp.bool_)
            ok_own = jnp.zeros(s_own.shape, jnp.bool_)
            for d in range(NSL):
                off = diag_ref[h * NSL + d]
                ok_prev = ok_prev | (rel_prev == off)
                ok_own = ok_own | ((rel_own == off) & ((off > 0) | (col_o <= row_o)))
        else:
            s_side = scores(q, sk_ref[...])
            v_side = sv_ref[...]
            ok_side = jnp.ones(s_side.shape, jnp.bool_)
            ok_prev = col_p > row_p
            ok_own = col_o <= row_o
        m_side = jnp.max(jnp.where(ok_side, s_side, neg), axis=1, keepdims=True)
        m_prev = jnp.max(jnp.where(ok_prev, s_prev, neg), axis=1, keepdims=True)
        m_own = jnp.max(jnp.where(ok_own, s_own, neg), axis=1, keepdims=True)
        m = jnp.maximum(jnp.maximum(m_side, m_prev), m_own)
        e_side = jnp.where(ok_side, jnp.exp(s_side - m), 0.0)
        e_prev = jnp.where(ok_prev, jnp.exp(s_prev - m), 0.0)
        e_own = jnp.where(ok_own, jnp.exp(s_own - m), 0.0)
        total = (jnp.sum(e_side, axis=1, keepdims=True)
                 + jnp.sum(e_prev, axis=1, keepdims=True)
                 + jnp.sum(e_own, axis=1, keepdims=True))
        p_side = (e_side / total).astype(jnp.bfloat16)
        p_prev = (e_prev / total).astype(jnp.bfloat16)
        p_own = (e_own / total).astype(jnp.bfloat16)
        out = jnp.dot(p_side, v_side, preferred_element_type=jnp.float32)
        out = out + jnp.dot(p_prev, prev_ref[1, p0:p1, :], preferred_element_type=jnp.float32)
        out = out + jnp.dot(p_own, own_ref[1, 0:w_own, :], preferred_element_type=jnp.float32)
        o_ref[r0:r0 + half, :] = out.astype(o_ref.dtype)

    @pl.when(roles_ref[h] != 1)
    def _():
        for part in range(parts):
            one_half(part, False)

    @pl.when(roles_ref[h] == 1)
    def _():
        for part in range(parts):
            one_half(part, True)


def attend(roles_l, slot_l, count_l, diag_l, q_local, prev_kv, own_kv, side):
    rows = q_local.shape[0]
    heads = q_local.shape[1] // HEAD_SIZE
    vrows = VB * BLK
    sink_block = MAX_RETRIEVERS * vrows // SINK
    grid_spec = pltpu.PrefetchScalarGridSpec(
        num_scalar_prefetch=4,
        grid=(heads,),
        in_specs=[
            pl.BlockSpec((rows, HEAD_SIZE), lambda h, *_: (0, h)),
            pl.BlockSpec((2, rows, HEAD_SIZE), lambda h, *_: (0, 0, 0)),
            pl.BlockSpec((2, rows, HEAD_SIZE), lambda h, *_: (0, 0, 0)),
            pl.BlockSpec((None, vrows, HEAD_SIZE), lambda h, r, s, *_: (0, s[h], 0)),
            pl.BlockSpec((None, vrows, HEAD_SIZE), lambda h, r, s, *_: (1, s[h], 0)),
            pl.BlockSpec((None, SINK, HEAD_SIZE), lambda h, *_: (0, sink_block, 0)),
            pl.BlockSpec((None, SINK, HEAD_SIZE), lambda h, *_: (1, sink_block, 0)),
        ],
        out_specs=pl.BlockSpec((rows, HEAD_SIZE), lambda h, *_: (0, h)),
    )
    return pl.pallas_call(
        attend_kernel,
        grid_spec=grid_spec,
        out_shape=jax.ShapeDtypeStruct(q_local.shape, jnp.bfloat16),
    )(roles_l, slot_l, count_l, diag_l, q_local, prev_kv, own_kv, side, side, side, side)


def scatter_sum(block, seq_devices):
    flat = block.reshape(seq_devices, -1, block.shape[-1])
    mine = lax.all_to_all(flat, "seq", 0, 0, tiled=True)
    return jnp.sum(mine.astype(jnp.float32), 0, keepdims=True).astype(block.dtype)


def gather_sums(total, shape, seq_devices):
    every = lax.all_to_all(jnp.broadcast_to(total, (seq_devices,) + total.shape[1:]), "seq", 0, 0, tiled=True)
    return every.reshape(shape)


def shards(queries, keys, values, prefix_keys, prefix_values, roles, columns, col_count, diagonals):
    seq_devices = lax.axis_size("seq")
    my_seq = lax.axis_index("seq")
    cache_rows = prefix_keys.shape[0]
    blocks_dev = cache_rows // BLK
    heads = roles.shape[0]

    is_ret = roles == 1
    slot = jnp.cumsum(is_ret.astype(jnp.int32)) - 1
    match = is_ret[None, :] & (slot[None, :] == jnp.arange(MAX_RETRIEVERS, dtype=jnp.int32)[:, None])
    head_of_slot = jnp.argmax(match, axis=1)
    cols_s = columns[head_of_slot]
    owner = cols_s // blocks_dev
    local_block = cols_s - owner * blocks_dev
    mine = (owner == my_seq)[:, :, None, None]
    kv_blocks = jnp.stack([prefix_keys, prefix_values], 0).reshape(2, blocks_dev, BLK, HEAD_SIZE)
    pieces = kv_blocks[:, local_block]
    pieces = jnp.where(mine[None], pieces, jnp.zeros_like(pieces))
    pieces = pieces.reshape(2, MAX_RETRIEVERS * VB * BLK, HEAD_SIZE)
    sink = jnp.stack([prefix_keys[:SINK], prefix_values[:SINK]], 0)
    sink = jnp.where(my_seq == 0, sink, jnp.zeros_like(sink))
    both = jnp.concatenate([pieces, sink], 1)

    head_devices = lax.axis_size("head")
    my_head = lax.axis_index("head")
    q_width = queries.shape[1] // head_devices
    kv_width = keys.shape[1] // head_devices

    def columns_for(dest):
        q_part = lax.dynamic_slice_in_dim(queries, dest * q_width, q_width, 1)
        k_part = lax.dynamic_slice_in_dim(keys, dest * kv_width, kv_width, 1)
        v_part = lax.dynamic_slice_in_dim(values, dest * kv_width, kv_width, 1)
        return jnp.concatenate([q_part, k_part, v_part], 1)

    received = [columns_for(my_head)]
    for k in range(1, head_devices):
        received.append(shifted(columns_for((my_head + k) % head_devices), "head", k))
    total = scatter_sum(both, seq_devices)
    total, received = lax.optimization_barrier((total, received))
    by_shift = jnp.stack(received, 0)
    order = (my_head - jnp.arange(head_devices, dtype=jnp.int32)) % head_devices
    tokens = by_shift[order].reshape(-1, q_width + 2 * kv_width)
    q_local = tokens[:, :q_width]
    kv_local = jnp.stack([tokens[:, q_width:q_width + kv_width], tokens[:, q_width + kv_width:]], 0)
    tail_cache = jnp.stack([prefix_keys[cache_rows - WIN:], prefix_values[cache_rows - WIN:]], 0)
    outgoing = jnp.where(my_seq == seq_devices - 1, tail_cache, kv_local)
    prev_kv = shifted(outgoing, "seq", 1)
    side = gather_sums(total, both.shape, seq_devices)

    slot_l = jnp.where(is_ret, slot, 0).astype(jnp.int32)
    return attend(
        roles.astype(jnp.int32),
        slot_l,
        col_count.astype(jnp.int32),
        diagonals.reshape(heads * NSL).astype(jnp.int32),
        q_local,
        prev_kv,
        kv_local,
        side,
    )


def solution(mesh):
    placed = (
        P(("seq", "head"), None),
        P(("seq", "head"), None),
        P(("seq", "head"), None),
        P("seq", "head"),
        P("seq", "head"),
        P("head"),
        P("head", None),
        P("head"),
        P("head", None),
    )
    return jax.shard_map(
        shards, mesh=mesh, in_specs=placed, out_specs=P("seq", "head"), check_vma=False
    )
```

```python
import functools
import math

import jax
import jax.numpy as jnp
from jax import lax
from jax.experimental import pallas as pl
from jax.experimental.pallas import tpu as pltpu
from jax.sharding import PartitionSpec as P

QUERY_HEADS = 64
KEY_VALUE_HEADS = 8
HEAD_SIZE = 128
SINK = 128
WIN = 512
BLK = 64
VB = 6
NSL = 4
MAX_RETRIEVERS = 4


def shifted(block, axis, distance):
    devices = range(lax.axis_size(axis))
    route = [((i - distance) % len(devices), i) for i in devices]
    return lax.ppermute(block, axis, route)


def attend_kernel(roles_ref, slot_ref, count_ref, diag_ref,
                  q_ref, prev_ref, own_ref, vk_ref, vv_ref, sk_ref, sv_ref, o_ref):
    h = pl.program_id(0)
    rows = q_ref.shape[0]
    half = rows // 2
    scaling = 1.0 / math.sqrt(HEAD_SIZE)
    dims = (((1,), (1,)), ((), ()))
    neg = -jnp.inf

    def scores(q, keys):
        return lax.dot_general(q, keys, dims, preferred_element_type=jnp.float32) * scaling

    def one_half(part, role_ret):
        r0 = part * half
        p0 = part * half
        p1 = rows
        w_own = half + part * half
        q = q_ref[r0:r0 + half, :]
        s_prev = scores(q, prev_ref[0, p0:p1, :])
        s_own = scores(q, own_ref[0, 0:w_own, :])
        row_p = lax.broadcasted_iota(jnp.int32, s_prev.shape, 0) + r0
        col_p = lax.broadcasted_iota(jnp.int32, s_prev.shape, 1) + p0
        row_o = lax.broadcasted_iota(jnp.int32, s_own.shape, 0) + r0
        col_o = lax.broadcasted_iota(jnp.int32, s_own.shape, 1)
        if role_ret:
            s_side = scores(q, vk_ref[...])
            v_side = vv_ref[...]
            side_col = lax.broadcasted_iota(jnp.int32, s_side.shape, 1)
            ok_side = side_col // BLK < count_ref[h]
            rel_prev = row_p // BLK + rows // BLK - col_p // BLK
            rel_own = row_o // BLK - col_o // BLK
            ok_prev = jnp.zeros(s_prev.shape, jnp.bool_)
            ok_own = jnp.zeros(s_own.shape, jnp.bool_)
            for d in range(NSL):
                off = diag_ref[h * NSL + d]
                ok_prev = ok_prev | (rel_prev == off)
                ok_own = ok_own | ((rel_own == off) & ((off > 0) | (col_o <= row_o)))
        else:
            s_side = scores(q, sk_ref[...])
            v_side = sv_ref[...]
            ok_side = jnp.ones(s_side.shape, jnp.bool_)
            ok_prev = col_p > row_p
            ok_own = col_o <= row_o
        m_side = jnp.max(jnp.where(ok_side, s_side, neg), axis=1, keepdims=True)
        m_prev = jnp.max(jnp.where(ok_prev, s_prev, neg), axis=1, keepdims=True)
        m_own = jnp.max(jnp.where(ok_own, s_own, neg), axis=1, keepdims=True)
        m = jnp.maximum(jnp.maximum(m_side, m_prev), m_own)
        e_side = jnp.where(ok_side, jnp.exp(s_side - m), 0.0)
        e_prev = jnp.where(ok_prev, jnp.exp(s_prev - m), 0.0)
        e_own = jnp.where(ok_own, jnp.exp(s_own - m), 0.0)
        total = (jnp.sum(e_side, axis=1, keepdims=True)
                 + jnp.sum(e_prev, axis=1, keepdims=True)
                 + jnp.sum(e_own, axis=1, keepdims=True))
        p_side = (e_side / total).astype(jnp.bfloat16)
        p_prev = (e_prev / total).astype(jnp.bfloat16)
        p_own = (e_own / total).astype(jnp.bfloat16)
        out = jnp.dot(p_side, v_side, preferred_element_type=jnp.float32)
        out = out + jnp.dot(p_prev, prev_ref[1, p0:p1, :], preferred_element_type=jnp.float32)
        out = out + jnp.dot(p_own, own_ref[1, 0:w_own, :], preferred_element_type=jnp.float32)
        o_ref[r0:r0 + half, :] = out.astype(o_ref.dtype)

    @pl.when(roles_ref[h] != 1)
    def _():
        one_half(0, False)
        one_half(1, False)

    @pl.when(roles_ref[h] == 1)
    def _():
        one_half(0, True)
        one_half(1, True)


def attend(roles_l, slot_l, count_l, diag_l, q_local, prev_kv, own_kv, side):
    rows = q_local.shape[0]
    heads = q_local.shape[1] // HEAD_SIZE
    vrows = VB * BLK
    sink_block = MAX_RETRIEVERS * vrows // SINK
    grid_spec = pltpu.PrefetchScalarGridSpec(
        num_scalar_prefetch=4,
        grid=(heads,),
        in_specs=[
            pl.BlockSpec((rows, HEAD_SIZE), lambda h, *_: (0, h)),
            pl.BlockSpec((2, rows, HEAD_SIZE), lambda h, *_: (0, 0, 0)),
            pl.BlockSpec((2, rows, HEAD_SIZE), lambda h, *_: (0, 0, 0)),
            pl.BlockSpec((None, vrows, HEAD_SIZE), lambda h, r, s, *_: (0, s[h], 0)),
            pl.BlockSpec((None, vrows, HEAD_SIZE), lambda h, r, s, *_: (1, s[h], 0)),
            pl.BlockSpec((None, SINK, HEAD_SIZE), lambda h, *_: (0, sink_block, 0)),
            pl.BlockSpec((None, SINK, HEAD_SIZE), lambda h, *_: (1, sink_block, 0)),
        ],
        out_specs=pl.BlockSpec((rows, HEAD_SIZE), lambda h, *_: (0, h)),
    )
    return pl.pallas_call(
        attend_kernel,
        grid_spec=grid_spec,
        out_shape=jax.ShapeDtypeStruct(q_local.shape, jnp.bfloat16),
    )(roles_l, slot_l, count_l, diag_l, q_local, prev_kv, own_kv, side, side, side, side)


def scatter_sum(block, seq_devices):
    flat = block.reshape(seq_devices, -1, block.shape[-1])
    mine = lax.all_to_all(flat, "seq", 0, 0, tiled=True)
    return jnp.sum(mine.astype(jnp.float32), 0, keepdims=True).astype(block.dtype)


def gather_sums(total, shape, seq_devices):
    every = lax.all_to_all(jnp.broadcast_to(total, (seq_devices,) + total.shape[1:]), "seq", 0, 0, tiled=True)
    return every.reshape(shape)


def shards(queries, keys, values, prefix_keys, prefix_values, roles, columns, col_count, diagonals):
    seq_devices = lax.axis_size("seq")
    my_seq = lax.axis_index("seq")
    cache_rows = prefix_keys.shape[0]
    blocks_dev = cache_rows // BLK
    heads = roles.shape[0]

    is_ret = roles == 1
    slot = jnp.cumsum(is_ret.astype(jnp.int32)) - 1
    match = is_ret[None, :] & (slot[None, :] == jnp.arange(MAX_RETRIEVERS, dtype=jnp.int32)[:, None])
    head_of_slot = jnp.argmax(match, axis=1)
    cols_s = columns[head_of_slot]
    owner = cols_s // blocks_dev
    local_block = cols_s - owner * blocks_dev
    mine = (owner == my_seq)[:, :, None, None]

    def held(cache):
        picked = cache.reshape(blocks_dev, BLK, HEAD_SIZE)[local_block]
        picked = jnp.where(mine, picked, jnp.zeros_like(picked)).reshape(-1, HEAD_SIZE)
        sink = jnp.where(my_seq == 0, cache[:SINK], jnp.zeros_like(cache[:SINK]))
        return jnp.concatenate([picked, sink], 0)

    both = jnp.stack([held(prefix_keys), held(prefix_values)], 0)

    head_devices = lax.axis_size("head")
    my_head = lax.axis_index("head")
    q_width = queries.shape[1] // head_devices
    kv_width = keys.shape[1] // head_devices

    def columns_for(dest):
        q_part = lax.dynamic_slice_in_dim(queries, dest * q_width, q_width, 1)
        k_part = lax.dynamic_slice_in_dim(keys, dest * kv_width, kv_width, 1)
        v_part = lax.dynamic_slice_in_dim(values, dest * kv_width, kv_width, 1)
        return jnp.concatenate([q_part, k_part, v_part], 1)

    received = [columns_for(my_head)]
    for k in range(1, head_devices):
        received.append(shifted(columns_for((my_head + k) % head_devices), "head", k))
    total = scatter_sum(both, seq_devices)
    total, received = lax.optimization_barrier((total, received))
    by_shift = jnp.stack(received, 0)
    order = (my_head - jnp.arange(head_devices, dtype=jnp.int32)) % head_devices
    tokens = by_shift[order].reshape(-1, q_width + 2 * kv_width)
    q_local = tokens[:, :q_width]
    kv_local = jnp.stack([tokens[:, q_width:q_width + kv_width], tokens[:, q_width + kv_width:]], 0)
    tail_cache = jnp.stack([prefix_keys[cache_rows - WIN:], prefix_values[cache_rows - WIN:]], 0)
    outgoing = jnp.where(my_seq == seq_devices - 1, tail_cache, kv_local)
    prev_kv = shifted(outgoing, "seq", 1)
    side = gather_sums(total, both.shape, seq_devices)

    slot_l = jnp.where(is_ret, slot, 0).astype(jnp.int32)
    return attend(
        roles.astype(jnp.int32),
        slot_l,
        col_count.astype(jnp.int32),
        diagonals.reshape(heads * NSL).astype(jnp.int32),
        q_local,
        prev_kv,
        kv_local,
        side,
    )


def solution(mesh):
    placed = (
        P(("seq", "head"), None),
        P(("seq", "head"), None),
        P(("seq", "head"), None),
        P("seq", "head"),
        P("seq", "head"),
        P("head"),
        P("head", None),
        P("head"),
        P("head", None),
    )
    return jax.shard_map(
        shards, mesh=mesh, in_specs=placed, out_specs=P("seq", "head"), check_vma=False
    )
```

```python
import functools
import math

import jax
import jax.numpy as jnp
from jax import lax
from jax.experimental import pallas as pl
from jax.experimental.pallas import tpu as pltpu
from jax.sharding import PartitionSpec as P

QUERY_HEADS = 64
KEY_VALUE_HEADS = 8
HEAD_SIZE = 128
SINK = 128
WIN = 512
BLK = 64
VB = 6
NSL = 4
MAX_RETRIEVERS = 4


def shifted(block, axis, distance):
    devices = range(lax.axis_size(axis))
    route = [((i - distance) % len(devices), i) for i in devices]
    return lax.ppermute(block, axis, route)


def attend_kernel(roles_ref, slot_ref, count_ref, diag_ref,
                  q_ref, prev_ref, own_ref, vk_ref, vv_ref, sk_ref, sv_ref, o_ref):
    h = pl.program_id(0)
    rows = q_ref.shape[0]
    half = rows // 2
    scaling = 1.0 / math.sqrt(HEAD_SIZE)
    dims = (((1,), (1,)), ((), ()))
    neg = -jnp.inf

    def scores(q, keys):
        return lax.dot_general(q, keys, dims, preferred_element_type=jnp.float32) * scaling

    def one_half(part, role_ret):
        r0 = part * half
        p0 = part * half
        p1 = rows
        w_own = half + part * half
        q = q_ref[r0:r0 + half, :]
        s_prev = scores(q, prev_ref[0, p0:p1, :])
        s_own = scores(q, own_ref[0, 0:w_own, :])
        row_p = lax.broadcasted_iota(jnp.int32, s_prev.shape, 0) + r0
        col_p = lax.broadcasted_iota(jnp.int32, s_prev.shape, 1) + p0
        row_o = lax.broadcasted_iota(jnp.int32, s_own.shape, 0) + r0
        col_o = lax.broadcasted_iota(jnp.int32, s_own.shape, 1)
        if role_ret:
            s_side = scores(q, vk_ref[...])
            v_side = vv_ref[...]
            side_col = lax.broadcasted_iota(jnp.int32, s_side.shape, 1)
            ok_side = side_col // BLK < count_ref[h]
            rel_prev = row_p // BLK + rows // BLK - col_p // BLK
            rel_own = row_o // BLK - col_o // BLK
            ok_prev = jnp.zeros(s_prev.shape, jnp.bool_)
            ok_own = jnp.zeros(s_own.shape, jnp.bool_)
            for d in range(NSL):
                off = diag_ref[h * NSL + d]
                ok_prev = ok_prev | (rel_prev == off)
                ok_own = ok_own | ((rel_own == off) & ((off > 0) | (col_o <= row_o)))
        else:
            s_side = scores(q, sk_ref[...])
            v_side = sv_ref[...]
            ok_side = jnp.ones(s_side.shape, jnp.bool_)
            ok_prev = col_p > row_p
            ok_own = col_o <= row_o
        m_side = jnp.max(jnp.where(ok_side, s_side, neg), axis=1, keepdims=True)
        m_prev = jnp.max(jnp.where(ok_prev, s_prev, neg), axis=1, keepdims=True)
        m_own = jnp.max(jnp.where(ok_own, s_own, neg), axis=1, keepdims=True)
        m = jnp.maximum(jnp.maximum(m_side, m_prev), m_own)
        e_side = jnp.where(ok_side, jnp.exp(s_side - m), 0.0)
        e_prev = jnp.where(ok_prev, jnp.exp(s_prev - m), 0.0)
        e_own = jnp.where(ok_own, jnp.exp(s_own - m), 0.0)
        total = (jnp.sum(e_side, axis=1, keepdims=True)
                 + jnp.sum(e_prev, axis=1, keepdims=True)
                 + jnp.sum(e_own, axis=1, keepdims=True))
        p_side = (e_side / total).astype(jnp.bfloat16)
        p_prev = (e_prev / total).astype(jnp.bfloat16)
        p_own = (e_own / total).astype(jnp.bfloat16)
        out = jnp.dot(p_side, v_side, preferred_element_type=jnp.float32)
        out = out + jnp.dot(p_prev, prev_ref[1, p0:p1, :], preferred_element_type=jnp.float32)
        out = out + jnp.dot(p_own, own_ref[1, 0:w_own, :], preferred_element_type=jnp.float32)
        o_ref[r0:r0 + half, :] = out.astype(o_ref.dtype)

    @pl.when(roles_ref[h] != 1)
    def _():
        one_half(0, False)
        one_half(1, False)

    @pl.when(roles_ref[h] == 1)
    def _():
        one_half(0, True)
        one_half(1, True)


def attend(roles_l, slot_l, count_l, diag_l, q_local, prev_kv, own_kv, side):
    rows = q_local.shape[0]
    heads = q_local.shape[1] // HEAD_SIZE
    vrows = VB * BLK
    sink_block = MAX_RETRIEVERS * vrows // SINK
    grid_spec = pltpu.PrefetchScalarGridSpec(
        num_scalar_prefetch=4,
        grid=(heads,),
        in_specs=[
            pl.BlockSpec((rows, HEAD_SIZE), lambda h, *_: (0, h)),
            pl.BlockSpec((2, rows, HEAD_SIZE), lambda h, *_: (0, 0, 0)),
            pl.BlockSpec((2, rows, HEAD_SIZE), lambda h, *_: (0, 0, 0)),
            pl.BlockSpec((None, vrows, HEAD_SIZE), lambda h, r, s, *_: (0, s[h], 0)),
            pl.BlockSpec((None, vrows, HEAD_SIZE), lambda h, r, s, *_: (1, s[h], 0)),
            pl.BlockSpec((None, SINK, HEAD_SIZE), lambda h, *_: (0, sink_block, 0)),
            pl.BlockSpec((None, SINK, HEAD_SIZE), lambda h, *_: (1, sink_block, 0)),
        ],
        out_specs=pl.BlockSpec((rows, HEAD_SIZE), lambda h, *_: (0, h)),
    )
    return pl.pallas_call(
        attend_kernel,
        grid_spec=grid_spec,
        out_shape=jax.ShapeDtypeStruct(q_local.shape, jnp.bfloat16),
    )(roles_l, slot_l, count_l, diag_l, q_local, prev_kv, own_kv, side, side, side, side)


def scatter_parts(block, seq_devices):
    flat = block.reshape(seq_devices, -1, block.shape[-1])
    return lax.all_to_all(flat, "seq", 0, 0, tiled=True)


def gather_sums(mine, shape, seq_devices):
    ones = jnp.ones((seq_devices, seq_devices), mine.dtype)
    total = jnp.einsum("ab,bcd->acd", ones, mine, preferred_element_type=jnp.float32).astype(mine.dtype)
    every = lax.all_to_all(total, "seq", 0, 0, tiled=True)
    return every.reshape(shape)


def shards(queries, keys, values, prefix_keys, prefix_values, roles, columns, col_count, diagonals):
    seq_devices = lax.axis_size("seq")
    my_seq = lax.axis_index("seq")
    cache_rows = prefix_keys.shape[0]
    blocks_dev = cache_rows // BLK
    heads = roles.shape[0]

    is_ret = roles == 1
    slot = jnp.cumsum(is_ret.astype(jnp.int32)) - 1
    match = is_ret[None, :] & (slot[None, :] == jnp.arange(MAX_RETRIEVERS, dtype=jnp.int32)[:, None])
    head_of_slot = jnp.argmax(match, axis=1)
    cols_s = columns[head_of_slot]
    owner = cols_s // blocks_dev
    local_block = cols_s - owner * blocks_dev
    mine = (owner == my_seq)[:, :, None, None]
    kv_blocks = jnp.stack([prefix_keys, prefix_values], 0).reshape(2, blocks_dev, BLK, HEAD_SIZE)
    pieces = kv_blocks[:, local_block]
    pieces = jnp.where(mine[None], pieces, jnp.zeros_like(pieces))
    pieces = pieces.reshape(2, MAX_RETRIEVERS * VB * BLK, HEAD_SIZE)
    sink = jnp.stack([prefix_keys[:SINK], prefix_values[:SINK]], 0)
    sink = jnp.where(my_seq == 0, sink, jnp.zeros_like(sink))
    both = jnp.concatenate([pieces, sink], 1)

    head_devices = lax.axis_size("head")
    my_head = lax.axis_index("head")
    q_width = queries.shape[1] // head_devices
    kv_width = keys.shape[1] // head_devices

    def columns_for(dest):
        q_part = lax.dynamic_slice_in_dim(queries, dest * q_width, q_width, 1)
        k_part = lax.dynamic_slice_in_dim(keys, dest * kv_width, kv_width, 1)
        v_part = lax.dynamic_slice_in_dim(values, dest * kv_width, kv_width, 1)
        return jnp.concatenate([q_part, k_part, v_part], 1)

    received = [columns_for(my_head)]
    for k in range(1, head_devices):
        received.append(shifted(columns_for((my_head + k) % head_devices), "head", k))
    mine = scatter_parts(both, seq_devices)
    mine, received = lax.optimization_barrier((mine, received))
    by_shift = jnp.stack(received, 0)
    order = (my_head - jnp.arange(head_devices, dtype=jnp.int32)) % head_devices
    tokens = by_shift[order].reshape(-1, q_width + 2 * kv_width)
    q_local = tokens[:, :q_width]
    kv_local = jnp.stack([tokens[:, q_width:q_width + kv_width], tokens[:, q_width + kv_width:]], 0)
    tail_cache = jnp.stack([prefix_keys[cache_rows - WIN:], prefix_values[cache_rows - WIN:]], 0)
    outgoing = jnp.where(my_seq == seq_devices - 1, tail_cache, kv_local)
    prev_kv = shifted(outgoing, "seq", 1)
    side = gather_sums(mine, both.shape, seq_devices)

    slot_l = jnp.where(is_ret, slot, 0).astype(jnp.int32)
    return attend(
        roles.astype(jnp.int32),
        slot_l,
        col_count.astype(jnp.int32),
        diagonals.reshape(heads * NSL).astype(jnp.int32),
        q_local,
        prev_kv,
        kv_local,
        side,
    )


def solution(mesh):
    placed = (
        P(("seq", "head"), None),
        P(("seq", "head"), None),
        P(("seq", "head"), None),
        P("seq", "head"),
        P("seq", "head"),
        P("head"),
        P("head", None),
        P("head"),
        P("head", None),
    )
    return jax.shard_map(
        shards, mesh=mesh, in_specs=placed, out_specs=P("seq", "head"), check_vma=False
    )
```

```python
import functools
import math

import jax
import jax.numpy as jnp
from jax import lax
from jax.experimental import pallas as pl
from jax.experimental.pallas import tpu as pltpu
from jax.sharding import PartitionSpec as P

QUERY_HEADS = 64
KEY_VALUE_HEADS = 8
HEAD_SIZE = 128
SINK = 128
WIN = 512
BLK = 64
VB = 6
NSL = 4
MAX_RETRIEVERS = 4


def shifted(block, axis, distance):
    devices = range(lax.axis_size(axis))
    route = [((i - distance) % len(devices), i) for i in devices]
    return lax.ppermute(block, axis, route)


def attend_kernel(roles_ref, slot_ref, count_ref, diag_ref,
                  q_ref, prev_ref, own_ref, vk_ref, vv_ref, sk_ref, sv_ref, o_ref):
    h = pl.program_id(0)
    rows = q_ref.shape[0]
    half = rows // 2
    scaling = 1.0 / math.sqrt(HEAD_SIZE)
    dims = (((1,), (1,)), ((), ()))
    neg = -jnp.inf

    def scores(q, keys):
        return lax.dot_general(q, keys, dims, preferred_element_type=jnp.float32) * scaling

    def one_half(part, role_ret):
        r0 = part * half
        p0 = part * half
        p1 = rows
        w_own = half + part * half
        q = q_ref[r0:r0 + half, :]
        s_prev = scores(q, prev_ref[0, p0:p1, :])
        s_own = scores(q, own_ref[0, 0:w_own, :])
        row_p = lax.broadcasted_iota(jnp.int32, s_prev.shape, 0) + r0
        col_p = lax.broadcasted_iota(jnp.int32, s_prev.shape, 1) + p0
        row_o = lax.broadcasted_iota(jnp.int32, s_own.shape, 0) + r0
        col_o = lax.broadcasted_iota(jnp.int32, s_own.shape, 1)
        if role_ret:
            s_side = scores(q, vk_ref[...])
            v_side = vv_ref[...]
            side_col = lax.broadcasted_iota(jnp.int32, s_side.shape, 1)
            ok_side = side_col // BLK < count_ref[h]
            rel_prev = row_p // BLK + rows // BLK - col_p // BLK
            rel_own = row_o // BLK - col_o // BLK
            ok_prev = jnp.zeros(s_prev.shape, jnp.bool_)
            ok_own = jnp.zeros(s_own.shape, jnp.bool_)
            for d in range(NSL):
                off = diag_ref[h * NSL + d]
                ok_prev = ok_prev | (rel_prev == off)
                ok_own = ok_own | ((rel_own == off) & ((off > 0) | (col_o <= row_o)))
        else:
            s_side = scores(q, sk_ref[...])
            v_side = sv_ref[...]
            ok_side = jnp.ones(s_side.shape, jnp.bool_)
            ok_prev = col_p > row_p
            ok_own = col_o <= row_o
        m_side = jnp.max(jnp.where(ok_side, s_side, neg), axis=1, keepdims=True)
        m_prev = jnp.max(jnp.where(ok_prev, s_prev, neg), axis=1, keepdims=True)
        m_own = jnp.max(jnp.where(ok_own, s_own, neg), axis=1, keepdims=True)
        m = jnp.maximum(jnp.maximum(m_side, m_prev), m_own)
        e_side = jnp.where(ok_side, jnp.exp(s_side - m), 0.0)
        e_prev = jnp.where(ok_prev, jnp.exp(s_prev - m), 0.0)
        e_own = jnp.where(ok_own, jnp.exp(s_own - m), 0.0)
        total = (jnp.sum(e_side, axis=1, keepdims=True)
                 + jnp.sum(e_prev, axis=1, keepdims=True)
                 + jnp.sum(e_own, axis=1, keepdims=True))
        p_side = (e_side / total).astype(jnp.bfloat16)
        p_prev = (e_prev / total).astype(jnp.bfloat16)
        p_own = (e_own / total).astype(jnp.bfloat16)
        out = jnp.dot(p_side, v_side, preferred_element_type=jnp.float32)
        out = out + jnp.dot(p_prev, prev_ref[1, p0:p1, :], preferred_element_type=jnp.float32)
        out = out + jnp.dot(p_own, own_ref[1, 0:w_own, :], preferred_element_type=jnp.float32)
        o_ref[r0:r0 + half, :] = out.astype(o_ref.dtype)

    @pl.when(roles_ref[h] != 1)
    def _():
        one_half(0, False)
        one_half(1, False)

    @pl.when(roles_ref[h] == 1)
    def _():
        one_half(0, True)
        one_half(1, True)


def attend(roles_l, slot_l, count_l, diag_l, q_local, prev_kv, own_kv, side):
    rows = q_local.shape[0]
    heads = q_local.shape[1] // HEAD_SIZE
    vrows = VB * BLK
    sink_block = MAX_RETRIEVERS * vrows // SINK
    grid_spec = pltpu.PrefetchScalarGridSpec(
        num_scalar_prefetch=4,
        grid=(heads,),
        in_specs=[
            pl.BlockSpec((rows, HEAD_SIZE), lambda h, *_: (0, h)),
            pl.BlockSpec((2, rows, HEAD_SIZE), lambda h, *_: (0, 0, 0)),
            pl.BlockSpec((2, rows, HEAD_SIZE), lambda h, *_: (0, 0, 0)),
            pl.BlockSpec((None, vrows, HEAD_SIZE), lambda h, r, s, *_: (0, s[h], 0)),
            pl.BlockSpec((None, vrows, HEAD_SIZE), lambda h, r, s, *_: (1, s[h], 0)),
            pl.BlockSpec((None, SINK, HEAD_SIZE), lambda h, *_: (0, sink_block, 0)),
            pl.BlockSpec((None, SINK, HEAD_SIZE), lambda h, *_: (1, sink_block, 0)),
        ],
        out_specs=pl.BlockSpec((rows, HEAD_SIZE), lambda h, *_: (0, h)),
    )
    return pl.pallas_call(
        attend_kernel,
        grid_spec=grid_spec,
        out_shape=jax.ShapeDtypeStruct(q_local.shape, jnp.bfloat16),
    )(roles_l, slot_l, count_l, diag_l, q_local, prev_kv, own_kv, side, side, side, side)


def scatter_parts(block, seq_devices):
    flat = block.reshape(seq_devices, -1, block.shape[-1])
    return lax.all_to_all(flat, "seq", 0, 0, tiled=True)


def gather_sums(mine, shape, seq_devices):
    ones = jnp.ones((seq_devices, seq_devices), mine.dtype)
    total = jnp.einsum("ab,bcd->acd", ones, mine, preferred_element_type=jnp.float32).astype(mine.dtype)
    every = lax.all_to_all(total, "seq", 0, 0, tiled=True)
    return every.reshape(shape)


def shards(queries, keys, values, prefix_keys, prefix_values, roles, columns, col_count, diagonals):
    seq_devices = lax.axis_size("seq")
    my_seq = lax.axis_index("seq")
    cache_rows = prefix_keys.shape[0]
    blocks_dev = cache_rows // BLK
    heads = roles.shape[0]

    is_ret = roles == 1
    slot = jnp.cumsum(is_ret.astype(jnp.int32)) - 1
    match = is_ret[None, :] & (slot[None, :] == jnp.arange(MAX_RETRIEVERS, dtype=jnp.int32)[:, None])
    head_of_slot = jnp.argmax(match, axis=1)
    cols_s = columns[head_of_slot]
    owner = cols_s // blocks_dev
    local_block = cols_s - owner * blocks_dev
    mine = owner == my_seq

    vrows = MAX_RETRIEVERS * VB * BLK
    half_rows = vrows + SINK
    r = jnp.arange(2 * half_rows, dtype=jnp.int32).reshape(seq_devices, -1)
    which, rr = r // half_rows, r % half_rows
    blk = jnp.minimum(rr // BLK, MAX_RETRIEVERS * VB - 1)
    in_vert = rr < vrows
    src = jnp.where(in_vert, local_block.reshape(-1)[blk] * BLK + rr % BLK, rr - vrows)
    valid = jnp.where(in_vert, mine.reshape(-1)[blk], my_seq == 0)
    table = jnp.concatenate([prefix_keys, prefix_values], 0)
    flat_both = table[which * cache_rows + src]
    flat_both = jnp.where(valid[:, :, None], flat_both, jnp.zeros_like(flat_both))
    both_shape = (2, half_rows, HEAD_SIZE)

    head_devices = lax.axis_size("head")
    my_head = lax.axis_index("head")
    q_width = queries.shape[1] // head_devices
    kv_width = keys.shape[1] // head_devices

    def columns_for(dest):
        q_part = lax.dynamic_slice_in_dim(queries, dest * q_width, q_width, 1)
        k_part = lax.dynamic_slice_in_dim(keys, dest * kv_width, kv_width, 1)
        v_part = lax.dynamic_slice_in_dim(values, dest * kv_width, kv_width, 1)
        return jnp.concatenate([q_part, k_part, v_part], 1)

    received = [columns_for(my_head)]
    for k in range(1, head_devices):
        received.append(shifted(columns_for((my_head + k) % head_devices), "head", k))
    mine = lax.all_to_all(flat_both, "seq", 0, 0, tiled=True)
    mine, received = lax.optimization_barrier((mine, received))
    by_shift = jnp.stack(received, 0)
    order = (my_head - jnp.arange(head_devices, dtype=jnp.int32)) % head_devices
    tokens = by_shift[order].reshape(-1, q_width + 2 * kv_width)
    q_local = tokens[:, :q_width]
    kv_local = jnp.stack([tokens[:, q_width:q_width + kv_width], tokens[:, q_width + kv_width:]], 0)
    tail_cache = jnp.stack([prefix_keys[cache_rows - WIN:], prefix_values[cache_rows - WIN:]], 0)
    outgoing = jnp.where(my_seq == seq_devices - 1, tail_cache, kv_local)
    prev_kv = shifted(outgoing, "seq", 1)
    side = gather_sums(mine, both_shape, seq_devices)

    slot_l = jnp.where(is_ret, slot, 0).astype(jnp.int32)
    return attend(
        roles.astype(jnp.int32),
        slot_l,
        col_count.astype(jnp.int32),
        diagonals.reshape(heads * NSL).astype(jnp.int32),
        q_local,
        prev_kv,
        kv_local,
        side,
    )


def solution(mesh):
    placed = (
        P(("seq", "head"), None),
        P(("seq", "head"), None),
        P(("seq", "head"), None),
        P("seq", "head"),
        P("seq", "head"),
        P("head"),
        P("head", None),
        P("head"),
        P("head", None),
    )
    return jax.shard_map(
        shards, mesh=mesh, in_specs=placed, out_specs=P("seq", "head"), check_vma=False
    )
```

```python
import functools
import math

import jax
import jax.numpy as jnp
from jax import lax
from jax.experimental import pallas as pl
from jax.experimental.pallas import tpu as pltpu
from jax.sharding import PartitionSpec as P

QUERY_HEADS = 64
KEY_VALUE_HEADS = 8
HEAD_SIZE = 128
SINK = 128
WIN = 512
BLK = 64
VB = 6
NSL = 4
MAX_RETRIEVERS = 4


def shifted(block, axis, distance):
    devices = range(lax.axis_size(axis))
    route = [((i - distance) % len(devices), i) for i in devices]
    return lax.ppermute(block, axis, route)


def attend_kernel(roles_ref, slot_ref, count_ref, diag_ref,
                  q_ref, prev_ref, own_ref, vk_ref, vv_ref, sk_ref, sv_ref, o_ref):
    h = pl.program_id(0)
    rows = q_ref.shape[0]
    half = rows // 2
    scaling = 1.0 / math.sqrt(HEAD_SIZE)
    dims = (((1,), (1,)), ((), ()))
    neg = -jnp.inf

    def scores(q, keys):
        return lax.dot_general(q, keys, dims, preferred_element_type=jnp.float32) * scaling

    def one_half(part, role_ret):
        r0 = part * half
        p0 = part * half
        p1 = rows
        w_own = half + part * half
        q = q_ref[r0:r0 + half, :]
        s_prev = scores(q, prev_ref[0, p0:p1, :])
        s_own = scores(q, own_ref[0, 0:w_own, :])
        row_p = lax.broadcasted_iota(jnp.int32, s_prev.shape, 0) + r0
        col_p = lax.broadcasted_iota(jnp.int32, s_prev.shape, 1) + p0
        row_o = lax.broadcasted_iota(jnp.int32, s_own.shape, 0) + r0
        col_o = lax.broadcasted_iota(jnp.int32, s_own.shape, 1)
        if role_ret:
            s_side = scores(q, vk_ref[...])
            v_side = vv_ref[...]
            side_col = lax.broadcasted_iota(jnp.int32, s_side.shape, 1)
            ok_side = side_col // BLK < count_ref[h]
            rel_prev = row_p // BLK + rows // BLK - col_p // BLK
            rel_own = row_o // BLK - col_o // BLK
            ok_prev = jnp.zeros(s_prev.shape, jnp.bool_)
            ok_own = jnp.zeros(s_own.shape, jnp.bool_)
            for d in range(NSL):
                off = diag_ref[h * NSL + d]
                ok_prev = ok_prev | (rel_prev == off)
                ok_own = ok_own | ((rel_own == off) & ((off > 0) | (col_o <= row_o)))
        else:
            s_side = scores(q, sk_ref[...])
            v_side = sv_ref[...]
            ok_side = jnp.ones(s_side.shape, jnp.bool_)
            ok_prev = col_p > row_p
            ok_own = col_o <= row_o
        m_side = jnp.max(jnp.where(ok_side, s_side, neg), axis=1, keepdims=True)
        m_prev = jnp.max(jnp.where(ok_prev, s_prev, neg), axis=1, keepdims=True)
        m_own = jnp.max(jnp.where(ok_own, s_own, neg), axis=1, keepdims=True)
        m = jnp.maximum(jnp.maximum(m_side, m_prev), m_own)
        e_side = jnp.where(ok_side, jnp.exp(s_side - m), 0.0)
        e_prev = jnp.where(ok_prev, jnp.exp(s_prev - m), 0.0)
        e_own = jnp.where(ok_own, jnp.exp(s_own - m), 0.0)
        total = (jnp.sum(e_side, axis=1, keepdims=True)
                 + jnp.sum(e_prev, axis=1, keepdims=True)
                 + jnp.sum(e_own, axis=1, keepdims=True))
        p_side = (e_side / total).astype(jnp.bfloat16)
        p_prev = (e_prev / total).astype(jnp.bfloat16)
        p_own = (e_own / total).astype(jnp.bfloat16)
        out = jnp.dot(p_side, v_side, preferred_element_type=jnp.float32)
        out = out + jnp.dot(p_prev, prev_ref[1, p0:p1, :], preferred_element_type=jnp.float32)
        out = out + jnp.dot(p_own, own_ref[1, 0:w_own, :], preferred_element_type=jnp.float32)
        o_ref[r0:r0 + half, :] = out.astype(o_ref.dtype)

    @pl.when(roles_ref[h] != 1)
    def _():
        one_half(0, False)
        one_half(1, False)

    @pl.when(roles_ref[h] == 1)
    def _():
        one_half(0, True)
        one_half(1, True)


def attend(roles_l, slot_l, count_l, diag_l, q_local, prev_kv, own_kv, side):
    rows = q_local.shape[0]
    heads = q_local.shape[1] // HEAD_SIZE
    vrows = VB * BLK
    sink_block = MAX_RETRIEVERS * vrows // SINK
    grid_spec = pltpu.PrefetchScalarGridSpec(
        num_scalar_prefetch=4,
        grid=(heads,),
        in_specs=[
            pl.BlockSpec((rows, HEAD_SIZE), lambda h, *_: (0, h)),
            pl.BlockSpec((2, rows, HEAD_SIZE), lambda h, *_: (0, 0, 0)),
            pl.BlockSpec((2, rows, HEAD_SIZE), lambda h, *_: (0, 0, 0)),
            pl.BlockSpec((None, vrows, HEAD_SIZE), lambda h, r, s, *_: (0, s[h], 0)),
            pl.BlockSpec((None, vrows, HEAD_SIZE), lambda h, r, s, *_: (1, s[h], 0)),
            pl.BlockSpec((None, SINK, HEAD_SIZE), lambda h, *_: (0, sink_block, 0)),
            pl.BlockSpec((None, SINK, HEAD_SIZE), lambda h, *_: (1, sink_block, 0)),
        ],
        out_specs=pl.BlockSpec((rows, HEAD_SIZE), lambda h, *_: (0, h)),
    )
    return pl.pallas_call(
        attend_kernel,
        grid_spec=grid_spec,
        out_shape=jax.ShapeDtypeStruct(q_local.shape, jnp.bfloat16),
    )(roles_l, slot_l, count_l, diag_l, q_local, prev_kv, own_kv, side, side, side, side)


def scatter_parts(block, seq_devices):
    flat = block.reshape(seq_devices, -1, block.shape[-1])
    return lax.all_to_all(flat, "seq", 0, 0, tiled=True)


def gather_sums(mine, shape, seq_devices):
    ones = jnp.ones((seq_devices, seq_devices), mine.dtype)
    total = jnp.einsum("ab,bcd->acd", ones, mine, preferred_element_type=jnp.float32).astype(mine.dtype)
    every = lax.all_to_all(total, "seq", 0, 0, tiled=True)
    return every.reshape(shape)


def shards(queries, keys, values, prefix_keys, prefix_values, roles, columns, col_count, diagonals):
    seq_devices = lax.axis_size("seq")
    my_seq = lax.axis_index("seq")
    cache_rows = prefix_keys.shape[0]
    blocks_dev = cache_rows // BLK
    heads = roles.shape[0]

    is_ret = roles == 1
    slot = jnp.cumsum(is_ret.astype(jnp.int32)) - 1
    match = is_ret[None, :] & (slot[None, :] == jnp.arange(MAX_RETRIEVERS, dtype=jnp.int32)[:, None])
    head_of_slot = jnp.argmax(match, axis=1)
    cols_s = columns[head_of_slot]
    owner = cols_s // blocks_dev
    local_block = cols_s - owner * blocks_dev
    sink_blocks = jnp.arange(SINK // BLK, dtype=jnp.int32)
    picks = jnp.concatenate([local_block.reshape(-1), sink_blocks])
    held = jnp.concatenate([(owner == my_seq).reshape(-1), jnp.broadcast_to(my_seq == 0, sink_blocks.shape)])
    kv_blocks = jnp.stack([prefix_keys, prefix_values], 0).reshape(2, blocks_dev, BLK, HEAD_SIZE)
    pieces = kv_blocks[:, picks]
    pieces = jnp.where(held[None, :, None, None], pieces, jnp.zeros_like(pieces))
    both = pieces.reshape(2, -1, HEAD_SIZE)

    head_devices = lax.axis_size("head")
    my_head = lax.axis_index("head")
    q_width = queries.shape[1] // head_devices
    kv_width = keys.shape[1] // head_devices

    def columns_for(dest):
        q_part = lax.dynamic_slice_in_dim(queries, dest * q_width, q_width, 1)
        k_part = lax.dynamic_slice_in_dim(keys, dest * kv_width, kv_width, 1)
        v_part = lax.dynamic_slice_in_dim(values, dest * kv_width, kv_width, 1)
        return jnp.concatenate([q_part, k_part, v_part], 1)

    received = [columns_for(my_head)]
    for k in range(1, head_devices):
        received.append(shifted(columns_for((my_head + k) % head_devices), "head", k))
    mine = scatter_parts(both, seq_devices)
    mine, received = lax.optimization_barrier((mine, received))
    by_shift = jnp.stack(received, 0)
    order = (my_head - jnp.arange(head_devices, dtype=jnp.int32)) % head_devices
    tokens = by_shift[order].reshape(-1, q_width + 2 * kv_width)
    q_local = tokens[:, :q_width]
    kv_local = jnp.stack([tokens[:, q_width:q_width + kv_width], tokens[:, q_width + kv_width:]], 0)
    tail_cache = jnp.stack([prefix_keys[cache_rows - WIN:], prefix_values[cache_rows - WIN:]], 0)
    outgoing = jnp.where(my_seq == seq_devices - 1, tail_cache, kv_local)
    prev_kv = shifted(outgoing, "seq", 1)
    side = gather_sums(mine, both.shape, seq_devices)

    slot_l = jnp.where(is_ret, slot, 0).astype(jnp.int32)
    return attend(
        roles.astype(jnp.int32),
        slot_l,
        col_count.astype(jnp.int32),
        diagonals.reshape(heads * NSL).astype(jnp.int32),
        q_local,
        prev_kv,
        kv_local,
        side,
    )


def solution(mesh):
    placed = (
        P(("seq", "head"), None),
        P(("seq", "head"), None),
        P(("seq", "head"), None),
        P("seq", "head"),
        P("seq", "head"),
        P("head"),
        P("head", None),
        P("head"),
        P("head", None),
    )
    return jax.shard_map(
        shards, mesh=mesh, in_specs=placed, out_specs=P("seq", "head"), check_vma=False
    )
```

```python
import functools
import math

import jax
import jax.numpy as jnp
from jax import lax
from jax.experimental import pallas as pl
from jax.experimental.pallas import tpu as pltpu
from jax.sharding import PartitionSpec as P

QUERY_HEADS = 64
KEY_VALUE_HEADS = 8
HEAD_SIZE = 128
SINK = 128
WIN = 512
BLK = 64
VB = 6
NSL = 4
MAX_RETRIEVERS = 4


def shifted(block, axis, distance):
    devices = range(lax.axis_size(axis))
    route = [((i - distance) % len(devices), i) for i in devices]
    return lax.ppermute(block, axis, route)


def attend_kernel(roles_ref, slot_ref, count_ref, diag_ref,
                  q_ref, prev_ref, own_ref, vk_ref, vv_ref, sk_ref, sv_ref, o_ref):
    h = pl.program_id(0)
    rows = q_ref.shape[0]
    half = rows // 2
    scaling = 1.0 / math.sqrt(HEAD_SIZE)
    dims = (((1,), (1,)), ((), ()))
    neg = -jnp.inf

    def scores(q, keys):
        return lax.dot_general(q, keys, dims, preferred_element_type=jnp.float32) * scaling

    def one_half(part, role_ret):
        r0 = part * half
        p0 = part * half
        p1 = rows
        w_own = half + part * half
        q = q_ref[r0:r0 + half, :]
        s_prev = scores(q, prev_ref[0, p0:p1, :])
        s_own = scores(q, own_ref[0, 0:w_own, :])
        row_p = lax.broadcasted_iota(jnp.int32, s_prev.shape, 0) + r0
        col_p = lax.broadcasted_iota(jnp.int32, s_prev.shape, 1) + p0
        row_o = lax.broadcasted_iota(jnp.int32, s_own.shape, 0) + r0
        col_o = lax.broadcasted_iota(jnp.int32, s_own.shape, 1)
        if role_ret:
            s_side = scores(q, vk_ref[...])
            v_side = vv_ref[...]
            side_col = lax.broadcasted_iota(jnp.int32, s_side.shape, 1)
            ok_side = side_col // BLK < count_ref[h]
            rel_prev = row_p // BLK + rows // BLK - col_p // BLK
            rel_own = row_o // BLK - col_o // BLK
            ok_prev = jnp.zeros(s_prev.shape, jnp.bool_)
            ok_own = jnp.zeros(s_own.shape, jnp.bool_)
            for d in range(NSL):
                off = diag_ref[h * NSL + d]
                ok_prev = ok_prev | (rel_prev == off)
                ok_own = ok_own | ((rel_own == off) & ((off > 0) | (col_o <= row_o)))
        else:
            s_side = scores(q, sk_ref[...])
            v_side = sv_ref[...]
            ok_side = jnp.ones(s_side.shape, jnp.bool_)
            ok_prev = col_p > row_p
            ok_own = col_o <= row_o
        m_side = jnp.max(jnp.where(ok_side, s_side, neg), axis=1, keepdims=True)
        m_prev = jnp.max(jnp.where(ok_prev, s_prev, neg), axis=1, keepdims=True)
        m_own = jnp.max(jnp.where(ok_own, s_own, neg), axis=1, keepdims=True)
        m = jnp.maximum(jnp.maximum(m_side, m_prev), m_own)
        e_side = jnp.where(ok_side, jnp.exp(s_side - m), 0.0)
        e_prev = jnp.where(ok_prev, jnp.exp(s_prev - m), 0.0)
        e_own = jnp.where(ok_own, jnp.exp(s_own - m), 0.0)
        total = (jnp.sum(e_side, axis=1, keepdims=True)
                 + jnp.sum(e_prev, axis=1, keepdims=True)
                 + jnp.sum(e_own, axis=1, keepdims=True))
        p_side = (e_side / total).astype(jnp.bfloat16)
        p_prev = (e_prev / total).astype(jnp.bfloat16)
        p_own = (e_own / total).astype(jnp.bfloat16)
        out = jnp.dot(p_side, v_side, preferred_element_type=jnp.float32)
        out = out + jnp.dot(p_prev, prev_ref[1, p0:p1, :], preferred_element_type=jnp.float32)
        out = out + jnp.dot(p_own, own_ref[1, 0:w_own, :], preferred_element_type=jnp.float32)
        o_ref[r0:r0 + half, :] = out.astype(o_ref.dtype)

    @pl.when(roles_ref[h] != 1)
    def _():
        one_half(0, False)
        one_half(1, False)

    @pl.when(roles_ref[h] == 1)
    def _():
        one_half(0, True)
        one_half(1, True)


def attend(roles_l, slot_l, count_l, diag_l, q_local, prev_kv, own_kv, side):
    rows = q_local.shape[0]
    heads = q_local.shape[1] // HEAD_SIZE
    vrows = VB * BLK
    sink_block = MAX_RETRIEVERS * vrows // SINK
    grid_spec = pltpu.PrefetchScalarGridSpec(
        num_scalar_prefetch=4,
        grid=(heads,),
        in_specs=[
            pl.BlockSpec((rows, HEAD_SIZE), lambda h, *_: (0, h)),
            pl.BlockSpec((2, rows, HEAD_SIZE), lambda h, *_: (0, 0, 0)),
            pl.BlockSpec((2, rows, HEAD_SIZE), lambda h, *_: (0, 0, 0)),
            pl.BlockSpec((None, vrows, HEAD_SIZE), lambda h, r, s, *_: (0, s[h], 0)),
            pl.BlockSpec((None, vrows, HEAD_SIZE), lambda h, r, s, *_: (1, s[h], 0)),
            pl.BlockSpec((None, SINK, HEAD_SIZE), lambda h, *_: (0, sink_block, 0)),
            pl.BlockSpec((None, SINK, HEAD_SIZE), lambda h, *_: (1, sink_block, 0)),
        ],
        out_specs=pl.BlockSpec((rows, HEAD_SIZE), lambda h, *_: (0, h)),
    )
    return pl.pallas_call(
        attend_kernel,
        grid_spec=grid_spec,
        out_shape=jax.ShapeDtypeStruct(q_local.shape, jnp.bfloat16),
    )(roles_l, slot_l, count_l, diag_l, q_local, prev_kv, own_kv, side, side, side, side)


def scatter_parts(block, seq_devices):
    flat = block.reshape(seq_devices, -1, block.shape[-1])
    return lax.all_to_all(flat, "seq", 0, 0, tiled=True)


def gather_sums(mine, shape, seq_devices):
    ones = jnp.ones((seq_devices, seq_devices), mine.dtype)
    total = jnp.einsum("ab,bcd->acd", ones, mine, preferred_element_type=jnp.float32).astype(mine.dtype)
    every = lax.all_to_all(total, "seq", 0, 0, tiled=True)
    return every.reshape(shape)


def shards(queries, keys, values, prefix_keys, prefix_values, roles, columns, col_count, diagonals):
    seq_devices = lax.axis_size("seq")
    my_seq = lax.axis_index("seq")
    cache_rows = prefix_keys.shape[0]
    blocks_dev = cache_rows // BLK
    heads = roles.shape[0]

    is_ret = roles == 1
    slot = jnp.cumsum(is_ret.astype(jnp.int32)) - 1
    match = is_ret[None, :] & (slot[None, :] == jnp.arange(MAX_RETRIEVERS, dtype=jnp.int32)[:, None])
    head_of_slot = jnp.argmax(match, axis=1)
    cols_s = columns[head_of_slot]
    owner = cols_s // blocks_dev
    local_block = cols_s - owner * blocks_dev
    sink_blocks = jnp.arange(SINK // BLK, dtype=jnp.int32)
    picks = jnp.concatenate([local_block.reshape(-1), sink_blocks])
    held = jnp.concatenate([(owner == my_seq).reshape(-1), jnp.broadcast_to(my_seq == 0, sink_blocks.shape)])
    pieces = jnp.stack([c.reshape(blocks_dev, BLK, HEAD_SIZE)[picks] for c in (prefix_keys, prefix_values)], 0)
    pieces = jnp.where(held[None, :, None, None], pieces, jnp.zeros_like(pieces))
    both = pieces.reshape(2, -1, HEAD_SIZE)

    head_devices = lax.axis_size("head")
    my_head = lax.axis_index("head")
    q_width = queries.shape[1] // head_devices
    kv_width = keys.shape[1] // head_devices

    def columns_for(dest):
        q_part = lax.dynamic_slice_in_dim(queries, dest * q_width, q_width, 1)
        k_part = lax.dynamic_slice_in_dim(keys, dest * kv_width, kv_width, 1)
        v_part = lax.dynamic_slice_in_dim(values, dest * kv_width, kv_width, 1)
        return jnp.concatenate([q_part, k_part, v_part], 1)

    received = [columns_for(my_head)]
    for k in range(1, head_devices):
        received.append(shifted(columns_for((my_head + k) % head_devices), "head", k))
    mine = scatter_parts(both, seq_devices)
    mine, received = lax.optimization_barrier((mine, received))
    by_shift = jnp.stack(received, 0)
    order = (my_head - jnp.arange(head_devices, dtype=jnp.int32)) % head_devices
    tokens = by_shift[order].reshape(-1, q_width + 2 * kv_width)
    q_local = tokens[:, :q_width]
    kv_local = jnp.stack([tokens[:, q_width:q_width + kv_width], tokens[:, q_width + kv_width:]], 0)
    tail_cache = jnp.stack([prefix_keys[cache_rows - WIN:], prefix_values[cache_rows - WIN:]], 0)
    outgoing = jnp.where(my_seq == seq_devices - 1, tail_cache, kv_local)
    prev_kv = shifted(outgoing, "seq", 1)
    side = gather_sums(mine, both.shape, seq_devices)

    slot_l = jnp.where(is_ret, slot, 0).astype(jnp.int32)
    return attend(
        roles.astype(jnp.int32),
        slot_l,
        col_count.astype(jnp.int32),
        diagonals.reshape(heads * NSL).astype(jnp.int32),
        q_local,
        prev_kv,
        kv_local,
        side,
    )


def solution(mesh):
    placed = (
        P(("seq", "head"), None),
        P(("seq", "head"), None),
        P(("seq", "head"), None),
        P("seq", "head"),
        P("seq", "head"),
        P("head"),
        P("head", None),
        P("head"),
        P("head", None),
    )
    return jax.shard_map(
        shards, mesh=mesh, in_specs=placed, out_specs=P("seq", "head"), check_vma=False
    )
```
